32 devices in a mesh: row: 4 (over y, core), col: 8 (over z, x).
Axes of the slice: x: 2, y: 2, z: 4, core: 2. Of those that a mesh axis runs over, the one named last changes fastest.
Arguments:
- solution: float32 [8, 32, 4096], P('col', None, 'row'), may hold values from -6 to 6
- residual: float32 [2, 4, 32, 4096], P(None, 'row', None, 'col'), may hold values from -6 to 6
- direction: float32 [8, 32, 4096], P('col', None, 'row'), may hold values from -6 to 6
- gradient: float32 [8, 32, 4096], P('col', None, 'row'), may hold values from -6 to 6
- left_factors: float32 [2, 4, 8, 4096, 128], P(None, 'row', 'col'), may hold values from -0.1875 to 0.1875
- right_factors: float32 [2, 4, 8, 4096, 128], P(None, 'row', 'col'), may hold values from -0.09375 to 0.09375
- ranks: int32 [2, 4, 8], P(None, 'row', 'col'), may hold values from 16 to 128, as said below
Outputs:
- solution_new: float32 [8, 32, 4096], P('col', None, 'row')
- residual_new: float32 [2, 4, 32, 4096], P(None, 'row', None, 'col')
- direction_new: float32 [8, 32, 4096], P('col', None, 'row')
- gradient_new: float32 [8, 32, 4096], P('col', None, 'row')
The draws below stay inside these ranges and needn't reach their ends.
Inputs may be any that keep to these rules, and one draw needn't show every extreme that they name: ranks tend to fall with the distance between a tile's row index round * 4 + block and its column index, but not monotonically (a noise of up to 4 is added); tiles on the diagonal have rank 128.
All inputs are finite; a program needn't handle non-finite values.
Results may differ from the reference program's by a relative error of at most 0.00012.
Values sent between devices are 32-bit elements; how exact they have to be, the bound alone decides.
No kernel may reach another device: no remote copies, remote signals or barrier semaphores. Data moves between devices by JAX's collectives and lax.ppermute only.
A program may use at most 64 MiB of HBM per device.

```python
import jax
import jax.numpy as jnp
from jax import lax

TILE = 4096
RMAX = 128
RHS = 32
ROUNDS = 2
ROW_BLOCKS = 4
TCOL = 8


def draw_ranks(key, part):
    rounds = jnp.arange(ROUNDS, dtype=jnp.int32)[:, None, None]
    blocks = jnp.arange(ROW_BLOCKS, dtype=jnp.int32)[None, :, None]
    columns = jnp.arange(TCOL, dtype=jnp.int32)[None, None, :]
    tile_row = rounds * ROW_BLOCKS + blocks
    distance = jnp.abs(tile_row - columns)
    lowest = RMAX // 8
    base = RMAX - distance * (RMAX - lowest) // max(TCOL - 1, 1)
    noise = jax.random.randint(key, (ROUNDS, ROW_BLOCKS, TCOL), -(RMAX // 16), RMAX // 16 + 1)
    value = jnp.clip(base + noise, lowest, RMAX)
    value = jnp.where(distance == 0, RMAX, value)
    value = jnp.where((tile_row == 0) & (columns == TCOL - 1), lowest, value)
    return value.astype(jnp.int32)


def level_of(key, dims, split, low, top_value):
    def one(dim, shards_of):
        steps = jax.random.uniform(jax.random.fold_in(jax.random.fold_in(key, 6), dim), (shards_of,), jnp.float32, low / len(split), top_value / len(split))
        return jnp.repeat(jnp.exp(steps), dims[dim] // shards_of).reshape((-1,) + (1,) * (len(dims) - dim - 1))

    gain = one(*split[0])
    for cut in split[1:]:
        gain = gain * one(*cut)
    return gain


def bell_draw(own_key, extent, width, most, shards=(), kind=jnp.bfloat16):
    entries = jax.random.normal(own_key, extent, jnp.float32) * width
    if len(shards) > 0:
        entries = level_of(own_key, extent, shards, -0.22, 0.18) * entries
    return jnp.clip(entries, min=-most, max=most).astype(kind)


def setup_inputs(seed: int = 0) -> dict:
    keys = jax.random.split(jax.random.key(seed), 8)
    solution = bell_draw(keys[0], (TCOL, RHS, TILE), 1.0, 6.0, ((0, 8), (2, 4)), jnp.float32)
    residual = bell_draw(keys[1], (ROUNDS, ROW_BLOCKS, RHS, TILE), 1.0, 6.0, ((1, 4), (3, 8)), jnp.float32)
    direction = bell_draw(keys[2], (TCOL, RHS, TILE), 1.0, 6.0, ((0, 8), (2, 4)), jnp.float32)
    gradient = bell_draw(keys[3], (TCOL, RHS, TILE), 1.0, 6.0, ((0, 8), (2, 4)), jnp.float32)
    left_factors = bell_draw(keys[4], (ROUNDS, ROW_BLOCKS, TCOL, TILE, RMAX), (RMAX * TCOL) ** -0.5, 0.1875, ((1, 4), (2, 8)), jnp.float32)
    right_factors = bell_draw(keys[5], (ROUNDS, ROW_BLOCKS, TCOL, TILE, RMAX), TILE ** -0.5, 0.09375, ((1, 4), (2, 8)), jnp.float32)
    ranks = draw_ranks(jax.random.fold_in(keys[7], 71), 0)
    return dict(solution=solution, residual=residual, direction=direction, gradient=gradient, left_factors=left_factors, right_factors=right_factors, ranks=ranks)


HIGH = lax.Precision.HIGHEST


def reference(solution, residual, direction, gradient, left_factors, right_factors, ranks):
    mask = (jnp.arange(RMAX, dtype=jnp.int32)[None, None, None, :] < ranks[..., None]).astype(jnp.float32)
    gamma = jnp.sum(gradient * gradient, axis=(0, 2))
    coeffs = jnp.einsum("chn,arcnm->archm", direction, right_factors, precision=HIGH) * mask[:, :, :, None, :]
    image = jnp.einsum("archm,arctm->arht", coeffs, left_factors, precision=HIGH)
    delta = jnp.sum(image * image, axis=(0, 1, 3))
    alpha = gamma / delta
    solution_new = solution + alpha[None, :, None] * direction
    residual_new = residual - alpha[None, None, :, None] * image
    back = jnp.einsum("arht,arctm->archm", residual_new, left_factors, precision=HIGH) * mask[:, :, :, None, :]
    gradient_new = jnp.einsum("archm,arcnm->chn", back, right_factors, precision=HIGH)
    beta = jnp.sum(gradient_new * gradient_new, axis=(0, 2)) / gamma
    direction_new = gradient_new + beta[None, :, None] * direction
    return (solution_new, residual_new, direction_new, gradient_new)
```

```python
import jax
import jax.numpy as jnp
from jax import lax
from jax.sharding import PartitionSpec as P

HIGH = lax.Precision.HIGHEST


def shards(solution, residual, direction, gradient, left_factors, right_factors, ranks):
    left = left_factors[:, 0, 0]
    right = right_factors[:, 0, 0]
    rounds, tile, rank_max = left.shape
    rhs = direction.shape[1]
    t_local = residual.shape[3]
    mask = (
        jnp.arange(rank_max, dtype=jnp.int32)[None, None, :] < ranks[:, 0, 0][:, None, None]
    ).astype(jnp.float32)
    residual_full = lax.all_gather(residual, "col", axis=3, tiled=True)[:, 0]
    g_local = jnp.sum(gradient * gradient, axis=(0, 2))
    coeffs = (
        jnp.einsum(
            "hn,anm->ahm",
            lax.all_gather(direction, "row", axis=2, tiled=True)[0],
            right,
            precision=HIGH,
        )
        * mask
    )
    partial_image = jnp.einsum("ahm,atm->aht", coeffs, left, precision=HIGH)
    extra = jnp.zeros((8, tile), jnp.float32).at[0, :rhs].set(g_local)
    payload = jnp.concatenate([partial_image.reshape(rounds * rhs, tile), extra], axis=0)
    summed = lax.psum(payload, "col")
    image_full = summed[: rounds * rhs].reshape(rounds, rhs, tile)
    gamma_col = summed[rounds * rhs, :rhs]
    d_local = jnp.sum(image_full * image_full, axis=(0, 2))
    sums = lax.psum(jnp.stack([gamma_col, d_local]), "row")
    gamma = sums[0]
    delta = sums[1]
    alpha = gamma / delta
    solution_new = solution + alpha[None, :, None] * direction
    residual_new_full = residual_full - alpha[None, :, None] * image_full
    c = lax.axis_index("col")
    image_mine = lax.dynamic_slice_in_dim(image_full, c * t_local, t_local, axis=2)
    residual_new = residual - alpha[None, None, :, None] * image_mine[:, None]
    back = jnp.einsum("aht,atm->ahm", residual_new_full, left, precision=HIGH) * mask
    partial_gradient = jnp.einsum("ahm,anm->hn", back, right, precision=HIGH)[None]
    gradient_new = lax.psum_scatter(partial_gradient, "row", scatter_dimension=2, tiled=True)
    g_new = lax.psum(lax.psum(jnp.sum(gradient_new * gradient_new, axis=(0, 2)), "row"), "col")
    beta = g_new / gamma
    direction_new = gradient_new + beta[None, :, None] * direction
    return (solution_new, residual_new, direction_new, gradient_new)


def solution(mesh):
    return jax.shard_map(
        shards,
        mesh=mesh,
        in_specs=(
            P("col", None, "row"),
            P(None, "row", None, "col"),
            P("col", None, "row"),
            P("col", None, "row"),
            P(None, "row", "col", None, None),
            P(None, "row", "col", None, None),
            P(None, "row", "col"),
        ),
        out_specs=(
            P("col", None, "row"),
            P(None, "row", None, "col"),
            P("col", None, "row"),
            P("col", None, "row"),
        ),
        check_vma=False,
    )
```

```python
import jax
import jax.numpy as jnp
from jax import lax
from jax.sharding import PartitionSpec as P

HIGH = lax.Precision.HIGHEST


def _steps(n):
    k = n.bit_length() - 1
    assert (1 << k) == n
    return k


def _partner(n, s):
    return [(i, i ^ (1 << s)) for i in range(n)]


def _bitrev(i, k):
    return int(format(i, f"0{k}b")[::-1], 2) if k else 0


def _halve(buf, axis, n, idx):
    for s in range(_steps(n)):
        bit = (idx >> s) & 1
        half = buf.shape[-1] // 2
        keep = lax.dynamic_slice_in_dim(buf, bit * half, half, axis=buf.ndim - 1)
        send = lax.dynamic_slice_in_dim(buf, (1 - bit) * half, half, axis=buf.ndim - 1)
        buf = keep + lax.ppermute(send, axis, _partner(n, s))
    return buf


def _double(buf, axis, n, idx, order):
    for s in order:
        bit = (idx >> s) & 1
        recv = lax.ppermute(buf, axis, _partner(n, s))
        buf = jnp.where(
            bit == 0,
            jnp.concatenate([buf, recv], axis=-1),
            jnp.concatenate([recv, buf], axis=-1),
        )
    return buf


def shards(solution, residual, direction, gradient, left_factors, right_factors, ranks):
    left = left_factors[:, 0, 0]
    right = right_factors[:, 0, 0]
    rounds, tile, rank_max = left.shape
    rhs = direction.shape[1]
    t_local = residual.shape[3]
    n_col = tile // t_local
    n_row = tile // direction.shape[2]
    c = lax.axis_index("col")
    r = lax.axis_index("row")
    mask = (
        jnp.arange(rank_max, dtype=jnp.int32)[None, None, :] < ranks[:, 0, 0][:, None, None]
    ).astype(jnp.float32)
    residual_full = _double(residual[:, 0], "col", n_col, c, range(_steps(n_col)))
    g_local = jnp.sum(gradient * gradient, axis=(0, 2))
    coeffs = (
        jnp.einsum(
            "hn,anm->ahm",
            lax.all_gather(direction, "row", axis=2, tiled=True)[0],
            right,
            precision=HIGH,
        )
        * mask
    )
    partial_image = jnp.einsum("ahm,atm->aht", coeffs, left, precision=HIGH)
    extra = jnp.zeros((8, tile), jnp.float32).at[0, :rhs].set(g_local)
    payload = jnp.concatenate([partial_image.reshape(rounds * rhs, tile), extra], axis=0)
    k_col = _steps(n_col)
    summed = _halve(payload, "col", n_col, c)
    summed = _double(summed, "col", n_col, c, reversed(range(k_col)))
    image_full = summed[: rounds * rhs].reshape(rounds, rhs, tile)
    gamma_col = summed[rounds * rhs, :rhs]
    d_local = jnp.sum(image_full * image_full, axis=(0, 2))
    sums = lax.psum(jnp.stack([gamma_col, d_local]), "row")
    gamma = sums[0]
    delta = sums[1]
    alpha = gamma / delta
    solution_new = solution + alpha[None, :, None] * direction
    residual_new_full = residual_full - alpha[None, :, None] * image_full
    image_mine = lax.dynamic_slice_in_dim(image_full, c * t_local, t_local, axis=2)
    residual_new = residual - alpha[None, None, :, None] * image_mine[:, None]
    back = jnp.einsum("aht,atm->ahm", residual_new_full, left, precision=HIGH) * mask
    partial_gradient = jnp.einsum("ahm,anm->hn", back, right, precision=HIGH)
    k_row = _steps(n_row)
    order = [_bitrev(p, k_row) for p in range(n_row)]
    blocks = partial_gradient.reshape(rhs, n_row, tile // n_row)[:, jnp.array(order)]
    gradient_new = _halve(blocks.reshape(rhs, tile), "row", n_row, r)[None]
    g_new = lax.psum(lax.psum(jnp.sum(gradient_new * gradient_new, axis=(0, 2)), "row"), "col")
    beta = g_new / gamma
    direction_new = gradient_new + beta[None, :, None] * direction
    return (solution_new, residual_new, direction_new, gradient_new)


def solution(mesh):
    return jax.shard_map(
        shards,
        mesh=mesh,
        in_specs=(
            P("col", None, "row"),
            P(None, "row", None, "col"),
            P("col", None, "row"),
            P("col", None, "row"),
            P(None, "row", "col", None, None),
            P(None, "row", "col", None, None),
            P(None, "row", "col"),
        ),
        out_specs=(
            P("col", None, "row"),
            P(None, "row", None, "col"),
            P("col", None, "row"),
            P("col", None, "row"),
        ),
        check_vma=False,
    )
```

```python
import jax
import jax.numpy as jnp
from jax import lax
from jax.sharding import PartitionSpec as P

HIGH = lax.Precision.HIGHEST


def _steps(n):
    k = n.bit_length() - 1
    assert (1 << k) == n
    return k


def _partner(n, s):
    return [(i, i ^ (1 << s)) for i in range(n)]


def _bitrev(i, k):
    return int(format(i, f"0{k}b")[::-1], 2) if k else 0


def _halve(buf, axis, n, idx):
    for s in range(_steps(n)):
        bit = (idx >> s) & 1
        half = buf.shape[-1] // 2
        keep = lax.dynamic_slice_in_dim(buf, bit * half, half, axis=buf.ndim - 1)
        send = lax.dynamic_slice_in_dim(buf, (1 - bit) * half, half, axis=buf.ndim - 1)
        buf = keep + lax.ppermute(send, axis, _partner(n, s))
    return buf


def _double(buf, axis, n, idx, order):
    for s in order:
        bit = (idx >> s) & 1
        recv = lax.ppermute(buf, axis, _partner(n, s))
        buf = jnp.where(
            bit == 0,
            jnp.concatenate([buf, recv], axis=-1),
            jnp.concatenate([recv, buf], axis=-1),
        )
    return buf


def _butterfly(x, axis, n):
    for s in range(_steps(n)):
        x = x + lax.ppermute(x, axis, _partner(n, s))
    return x


def shards(solution, residual, direction, gradient, left_factors, right_factors, ranks):
    left = left_factors[:, 0, 0]
    right = right_factors[:, 0, 0]
    rounds, tile, rank_max = left.shape
    rhs = direction.shape[1]
    t_local = residual.shape[3]
    n_col = tile // t_local
    n_row = tile // direction.shape[2]
    c = lax.axis_index("col")
    r = lax.axis_index("row")
    mask = (
        jnp.arange(rank_max, dtype=jnp.int32)[None, None, :] < ranks[:, 0, 0][:, None, None]
    ).astype(jnp.float32)
    residual_full = _double(residual[:, 0], "col", n_col, c, range(_steps(n_col)))
    g_local = jnp.sum(gradient * gradient, axis=(0, 2))
    coeffs = (
        jnp.einsum(
            "hn,anm->ahm",
            lax.all_gather(direction, "row", axis=2, tiled=True)[0],
            right,
            precision=HIGH,
        )
        * mask
    )
    partial_image = jnp.einsum("ahm,atm->aht", coeffs, left, precision=HIGH)
    extra = jnp.zeros((8, tile), jnp.float32).at[0, :rhs].set(g_local)
    payload = jnp.concatenate([partial_image.reshape(rounds * rhs, tile), extra], axis=0)
    k_col = _steps(n_col)
    summed = _halve(payload, "col", n_col, c)
    summed = _double(summed, "col", n_col, c, reversed(range(k_col)))
    image_full = summed[: rounds * rhs].reshape(rounds, rhs, tile)
    gamma_col = summed[rounds * rhs, :rhs]
    d_local = jnp.sum(image_full * image_full, axis=(0, 2))
    sums = _butterfly(jnp.stack([gamma_col, d_local]), "row", n_row)
    gamma = sums[0]
    delta = sums[1]
    alpha = gamma / delta
    solution_new = solution + alpha[None, :, None] * direction
    image_mine = lax.dynamic_slice_in_dim(image_full, c * t_local, t_local, axis=2)
    residual_new = residual - alpha[None, None, :, None] * image_mine[:, None]
    back_res = jnp.einsum("aht,atm->ahm", residual_full, left, precision=HIGH) * mask
    back_img = jnp.einsum("aht,atm->ahm", image_full, left, precision=HIGH) * mask
    back = back_res - alpha[None, :, None] * back_img
    partial_gradient = jnp.einsum("ahm,anm->hn", back, right, precision=HIGH)
    k_row = _steps(n_row)
    order = [_bitrev(p, k_row) for p in range(n_row)]
    blocks = partial_gradient.reshape(rhs, n_row, tile // n_row)[:, jnp.array(order)]
    gradient_new = _halve(blocks.reshape(rhs, tile), "row", n_row, r)[None]
    g_new = _butterfly(_butterfly(jnp.sum(gradient_new * gradient_new, axis=(0, 2)), "row", n_row), "col", n_col)
    beta = g_new / gamma
    direction_new = gradient_new + beta[None, :, None] * direction
    return (solution_new, residual_new, direction_new, gradient_new)


def solution(mesh):
    return jax.shard_map(
        shards,
        mesh=mesh,
        in_specs=(
            P("col", None, "row"),
            P(None, "row", None, "col"),
            P("col", None, "row"),
            P("col", None, "row"),
            P(None, "row", "col", None, None),
            P(None, "row", "col", None, None),
            P(None, "row", "col"),
        ),
        out_specs=(
            P("col", None, "row"),
            P(None, "row", None, "col"),
            P("col", None, "row"),
            P("col", None, "row"),
        ),
        check_vma=False,
    )
```

```python
import jax
import jax.numpy as jnp
from jax import lax
from jax.sharding import PartitionSpec as P

HIGH = lax.Precision.HIGHEST


def _steps(n):
    k = n.bit_length() - 1
    assert (1 << k) == n
    return k


def _partner(n, s):
    return [(i, i ^ (1 << s)) for i in range(n)]


def _bitrev(i, k):
    return int(format(i, f"0{k}b")[::-1], 2) if k else 0


def _join(bit, mine, theirs):
    return jnp.where(
        bit == 0,
        jnp.concatenate([mine, theirs], axis=0),
        jnp.concatenate([theirs, mine], axis=0),
    )


def _halve(buf, axis, n, idx):
    for s in range(_steps(n)):
        bit = (idx >> s) & 1
        half = buf.shape[-1] // 2
        keep = lax.dynamic_slice_in_dim(buf, bit * half, half, axis=buf.ndim - 1)
        send = lax.dynamic_slice_in_dim(buf, (1 - bit) * half, half, axis=buf.ndim - 1)
        buf = keep + lax.ppermute(send, axis, _partner(n, s))
    return buf


def _butterfly(x, axis, n):
    for s in range(_steps(n)):
        x = x + lax.ppermute(x, axis, _partner(n, s))
    return x


def _all_reduce_with_gather(buf, res, axis, n, idx):
    k = _steps(n)
    width = buf.shape[-1]
    for s in range(k):
        bit = (idx >> s) & 1
        half = buf.shape[0] // 2
        keep = lax.dynamic_slice_in_dim(buf, bit * half, half, axis=0)
        send = lax.dynamic_slice_in_dim(buf, (1 - bit) * half, half, axis=0)
        cut = send.size // width
        msg = jnp.concatenate([send.reshape(cut, width), res.reshape(-1, width)], axis=0)
        got = lax.ppermute(msg, axis, _partner(n, s))
        buf = keep + got[:cut].reshape(send.shape)
        res = _join(bit, res, got[cut:].reshape(res.shape))
    for s in reversed(range(k)):
        bit = (idx >> s) & 1
        buf = _join(bit, buf, lax.ppermute(buf, axis, _partner(n, s)))
    return buf, res


def shards(solution, residual, direction, gradient, left_factors, right_factors, ranks):
    left = left_factors[:, 0, 0]
    right = right_factors[:, 0, 0]
    rounds, tile, rank_max = left.shape
    rhs = direction.shape[1]
    t_local = residual.shape[3]
    n_col = tile // t_local
    n_row = tile // direction.shape[2]
    c = lax.axis_index("col")
    r = lax.axis_index("row")
    mask = (
        jnp.arange(rank_max, dtype=jnp.int32)[None, None, :] < ranks[:, 0, 0][:, None, None]
    ).astype(jnp.float32)
    left_blocks = left.reshape(rounds, n_col, t_local, rank_max)
    g_local = jnp.sum(gradient * gradient, axis=(0, 2))
    coeffs = (
        jnp.einsum(
            "hn,anm->ahm",
            lax.all_gather(direction, "row", axis=2, tiled=True)[0],
            right,
            precision=HIGH,
        )
        * mask
    )
    partial_image = jnp.einsum("ahm,ajtm->jaht", coeffs, left_blocks, precision=HIGH)
    extra = jnp.zeros((n_col, 8, t_local), jnp.float32).at[0, 0, :rhs].set(g_local)
    payload = jnp.concatenate(
        [partial_image.reshape(n_col, rounds * rhs, t_local), extra], axis=1
    )
    summed, residual_blocks = _all_reduce_with_gather(
        payload, residual[:, 0].reshape(1, rounds * rhs, t_local), "col", n_col, c
    )
    image_blocks = summed[:, : rounds * rhs].reshape(n_col, rounds, rhs, t_local)
    residual_blocks = residual_blocks.reshape(n_col, rounds, rhs, t_local)
    gamma_col = summed[0, rounds * rhs, :rhs]
    d_local = jnp.sum(image_blocks * image_blocks, axis=(0, 1, 3))
    sums = _butterfly(jnp.stack([gamma_col, d_local]), "row", n_row)
    gamma = sums[0]
    delta = sums[1]
    alpha = gamma / delta
    solution_new = solution + alpha[None, :, None] * direction
    image_mine = lax.dynamic_index_in_dim(image_blocks, c, 0, keepdims=False)
    residual_new = residual - alpha[None, None, :, None] * image_mine[:, None]
    back_res = jnp.einsum("jaht,ajtm->ahm", residual_blocks, left_blocks, precision=HIGH) * mask
    back_img = jnp.einsum("jaht,ajtm->ahm", image_blocks, left_blocks, precision=HIGH) * mask
    back = back_res - alpha[None, :, None] * back_img
    partial_gradient = jnp.einsum("ahm,anm->hn", back, right, precision=HIGH)
    k_row = _steps(n_row)
    order = [_bitrev(p, k_row) for p in range(n_row)]
    blocks = partial_gradient.reshape(rhs, n_row, tile // n_row)[:, jnp.array(order)]
    gradient_new = _halve(blocks.reshape(rhs, tile), "row", n_row, r)[None]
    g_new = _butterfly(
        _butterfly(jnp.sum(gradient_new * gradient_new, axis=(0, 2)), "row", n_row), "col", n_col
    )
    beta = g_new / gamma
    direction_new = gradient_new + beta[None, :, None] * direction
    return (solution_new, residual_new, direction_new, gradient_new)


def solution(mesh):
    return jax.shard_map(
        shards,
        mesh=mesh,
        in_specs=(
            P("col", None, "row"),
            P(None, "row", None, "col"),
            P("col", None, "row"),
            P("col", None, "row"),
            P(None, "row", "col", None, None),
            P(None, "row", "col", None, None),
            P(None, "row", "col"),
        ),
        out_specs=(
            P("col", None, "row"),
            P(None, "row", None, "col"),
            P("col", None, "row"),
            P("col", None, "row"),
        ),
        check_vma=False,
    )
```

```python
import jax
import jax.numpy as jnp
from jax import lax
from jax.sharding import PartitionSpec as P

HIGH = lax.Precision.HIGHEST


def _steps(n):
    k = n.bit_length() - 1
    assert (1 << k) == n
    return k


def _partner(n, s):
    return [(i, i ^ (1 << s)) for i in range(n)]


def _bitrev(i, k):
    return int(format(i, f"0{k}b")[::-1], 2) if k else 0


def _halve(buf, axis, n, idx):
    return _halve_from(buf, axis, n, idx, 0)


def _halve_from(buf, axis, n, idx, first):
    for s in range(first, _steps(n)):
        bit = (idx >> s) & 1
        half = buf.shape[-1] // 2
        keep = lax.dynamic_slice_in_dim(buf, bit * half, half, axis=buf.ndim - 1)
        send = lax.dynamic_slice_in_dim(buf, (1 - bit) * half, half, axis=buf.ndim - 1)
        buf = keep + lax.ppermute(send, axis, _partner(n, s))
    return buf


def _double(buf, axis, n, idx, order):
    for s in order:
        bit = (idx >> s) & 1
        recv = lax.ppermute(buf, axis, _partner(n, s))
        buf = jnp.where(
            bit == 0,
            jnp.concatenate([buf, recv], axis=-1),
            jnp.concatenate([recv, buf], axis=-1),
        )
    return buf


def _butterfly(x, axis, n):
    for s in range(_steps(n)):
        x = x + lax.ppermute(x, axis, _partner(n, s))
    return x


def shards(solution, residual, direction, gradient, left_factors, right_factors, ranks):
    left = left_factors[:, 0, 0]
    right = right_factors[:, 0, 0]
    rounds, tile, rank_max = left.shape
    rhs = direction.shape[1]
    t_local = residual.shape[3]
    n_col = tile // t_local
    n_row = tile // direction.shape[2]
    c = lax.axis_index("col")
    r = lax.axis_index("row")
    mask = (
        jnp.arange(rank_max, dtype=jnp.int32)[None, None, :] < ranks[:, 0, 0][:, None, None]
    ).astype(jnp.float32)
    g_local = jnp.sum(gradient * gradient, axis=(0, 2))
    coeffs = (
        jnp.einsum(
            "hn,anm->ahm",
            lax.all_gather(direction, "row", axis=2, tiled=True)[0],
            right,
            precision=HIGH,
        )
        * mask
    )
    partial_image = jnp.einsum("ahm,atm->aht", coeffs, left, precision=HIGH)
    extra = jnp.zeros((8, tile), jnp.float32).at[0, :rhs].set(g_local)
    payload = jnp.concatenate([partial_image.reshape(rounds * rhs, tile), extra], axis=0)
    k_col = _steps(n_col)
    res = residual[:, 0]
    res = _double(res, "col", n_col, c, range(k_col - 1))
    res, payload = lax.optimization_barrier((res, payload))
    bit = (c >> 0) & 1
    half = payload.shape[-1] // 2
    keep = lax.dynamic_slice_in_dim(payload, bit * half, half, axis=1)
    send = lax.dynamic_slice_in_dim(payload, (1 - bit) * half, half, axis=1)
    got = lax.ppermute(send, "col", _partner(n_col, 0))
    residual_full = _double(res, "col", n_col, c, range(k_col - 1, k_col))
    residual_full, got = lax.optimization_barrier((residual_full, got))
    summed = _halve_from(keep + got, "col", n_col, c, 1)
    summed = _double(summed, "col", n_col, c, reversed(range(k_col)))
    image_full = summed[: rounds * rhs].reshape(rounds, rhs, tile)
    gamma_col = summed[rounds * rhs, :rhs]
    d_local = jnp.sum(image_full * image_full, axis=(0, 2))
    sums = _butterfly(jnp.stack([gamma_col, d_local]), "row", n_row)
    gamma = sums[0]
    delta = sums[1]
    alpha = gamma / delta
    solution_new = solution + alpha[None, :, None] * direction
    image_mine = lax.dynamic_slice_in_dim(image_full, c * t_local, t_local, axis=2)
    residual_new = residual - alpha[None, None, :, None] * image_mine[:, None]
    back_res = jnp.einsum("aht,atm->ahm", residual_full, left, precision=HIGH) * mask
    back_img = jnp.einsum("aht,atm->ahm", image_full, left, precision=HIGH) * mask
    back = back_res - alpha[None, :, None] * back_img
    partial_gradient = jnp.einsum("ahm,anm->hn", back, right, precision=HIGH)
    k_row = _steps(n_row)
    order = [_bitrev(p, k_row) for p in range(n_row)]
    blocks = partial_gradient.reshape(rhs, n_row, tile // n_row)[:, jnp.array(order)]
    gradient_new = _halve(blocks.reshape(rhs, tile), "row", n_row, r)[None]
    g_new = _butterfly(_butterfly(jnp.sum(gradient_new * gradient_new, axis=(0, 2)), "row", n_row), "col", n_col)
    beta = g_new / gamma
    direction_new = gradient_new + beta[None, :, None] * direction
    return (solution_new, residual_new, direction_new, gradient_new)


def solution(mesh):
    return jax.shard_map(
        shards,
        mesh=mesh,
        in_specs=(
            P("col", None, "row"),
            P(None, "row", None, "col"),
            P("col", None, "row"),
            P("col", None, "row"),
            P(None, "row", "col", None, None),
            P(None, "row", "col", None, None),
            P(None, "row", "col"),
        ),
        out_specs=(
            P("col", None, "row"),
            P(None, "row", None, "col"),
            P("col", None, "row"),
            P("col", None, "row"),
        ),
        check_vma=False,
    )
```

```python
import jax
import jax.numpy as jnp
from jax import lax
from jax.sharding import PartitionSpec as P

HIGH = lax.Precision.HIGHEST


def _steps(n):
    k = n.bit_length() - 1
    assert (1 << k) == n
    return k


def _partner(n, s):
    return [(i, i ^ (1 << s)) for i in range(n)]


def _bitrev(i, k):
    return int(format(i, f"0{k}b")[::-1], 2) if k else 0


def _halve(buf, axis, n, idx):
    return _halve_from(buf, axis, n, idx, 0)


def _halve_from(buf, axis, n, idx, first, side=None):
    for s in range(first, _steps(n)):
        bit = (idx >> s) & 1
        half = buf.shape[-1] // 2
        keep = lax.dynamic_slice_in_dim(buf, bit * half, half, axis=buf.ndim - 1)
        send = lax.dynamic_slice_in_dim(buf, (1 - bit) * half, half, axis=buf.ndim - 1)
        if side is not None and s == first + 1:
            send, side = lax.optimization_barrier((send, side))
        buf = keep + lax.ppermute(send, axis, _partner(n, s))
    if side is not None:
        return buf, side
    return buf


def _double(buf, axis, n, idx, order):
    for s in order:
        bit = (idx >> s) & 1
        recv = lax.ppermute(buf, axis, _partner(n, s))
        buf = jnp.where(
            bit == 0,
            jnp.concatenate([buf, recv], axis=-1),
            jnp.concatenate([recv, buf], axis=-1),
        )
    return buf


def _butterfly(x, axis, n):
    for s in range(_steps(n)):
        x = x + lax.ppermute(x, axis, _partner(n, s))
    return x


def shards(solution, residual, direction, gradient, left_factors, right_factors, ranks):
    left = left_factors[:, 0, 0]
    right = right_factors[:, 0, 0]
    rounds, tile, rank_max = left.shape
    rhs = direction.shape[1]
    t_local = residual.shape[3]
    n_col = tile // t_local
    n_row = tile // direction.shape[2]
    c = lax.axis_index("col")
    r = lax.axis_index("row")
    mask = (
        jnp.arange(rank_max, dtype=jnp.int32)[None, None, :] < ranks[:, 0, 0][:, None, None]
    ).astype(jnp.float32)
    g_local = jnp.sum(gradient * gradient, axis=(0, 2))
    coeffs = (
        jnp.einsum(
            "hn,anm->ahm",
            lax.all_gather(direction, "row", axis=2, tiled=True)[0],
            right,
            precision=HIGH,
        )
        * mask
    )
    partial_image = jnp.einsum("ahm,atm->aht", coeffs, left, precision=HIGH)
    extra = jnp.zeros((8, tile), jnp.float32).at[0, :rhs].set(g_local)
    payload = jnp.concatenate([partial_image.reshape(rounds * rhs, tile), extra], axis=0)
    k_col = _steps(n_col)
    res_order = [2, 0, 1] + list(range(3, k_col)) if k_col >= 3 else list(range(k_col))
    res = residual[:, 0]
    res = _double(res, "col", n_col, c, res_order[:-1])
    res, payload = lax.optimization_barrier((res, payload))
    bit = (c >> 0) & 1
    half = payload.shape[-1] // 2
    keep = lax.dynamic_slice_in_dim(payload, bit * half, half, axis=1)
    send = lax.dynamic_slice_in_dim(payload, (1 - bit) * half, half, axis=1)
    got = lax.ppermute(send, "col", _partner(n_col, 0))
    res = _double(res, "col", n_col, c, res_order[-1:])
    res, got = lax.optimization_barrier((res, got))
    where = [sum(((d >> s) & 1) << i for i, s in enumerate(res_order)) for d in range(n_col)]
    residual_full = res.reshape(rounds, rhs, n_col, t_local)[:, :, jnp.array(where)]
    residual_full = residual_full.reshape(rounds, rhs, tile)
    back_res = jnp.einsum("aht,atm->ahm", residual_full, left, precision=HIGH) * mask
    summed = _halve_from(keep + got, "col", n_col, c, 1, back_res)
    back_res = summed[1]
    summed = _double(summed[0], "col", n_col, c, reversed(range(k_col)))
    image_full = summed[: rounds * rhs].reshape(rounds, rhs, tile)
    gamma_col = summed[rounds * rhs, :rhs]
    d_local = jnp.sum(image_full * image_full, axis=(0, 2))
    sums = _butterfly(jnp.stack([gamma_col, d_local]), "row", n_row)
    gamma = sums[0]
    delta = sums[1]
    alpha = gamma / delta
    solution_new = solution + alpha[None, :, None] * direction
    image_mine = lax.dynamic_slice_in_dim(image_full, c * t_local, t_local, axis=2)
    residual_new = residual - alpha[None, None, :, None] * image_mine[:, None]
    back_img = jnp.einsum("aht,atm->ahm", image_full, left, precision=HIGH) * mask
    back = back_res - alpha[None, :, None] * back_img
    partial_gradient = jnp.einsum("ahm,anm->hn", back, right, precision=HIGH)
    k_row = _steps(n_row)
    order = [_bitrev(p, k_row) for p in range(n_row)]
    blocks = partial_gradient.reshape(rhs, n_row, tile // n_row)[:, jnp.array(order)]
    gradient_new = _halve(blocks.reshape(rhs, tile), "row", n_row, r)[None]
    g_new = _butterfly(_butterfly(jnp.sum(gradient_new * gradient_new, axis=(0, 2)), "row", n_row), "col", n_col)
    beta = g_new / gamma
    direction_new = gradient_new + beta[None, :, None] * direction
    return (solution_new, residual_new, direction_new, gradient_new)


def solution(mesh):
    return jax.shard_map(
        shards,
        mesh=mesh,
        in_specs=(
            P("col", None, "row"),
            P(None, "row", None, "col"),
            P("col", None, "row"),
            P("col", None, "row"),
            P(None, "row", "col", None, None),
            P(None, "row", "col", None, None),
            P(None, "row", "col"),
        ),
        out_specs=(
            P("col", None, "row"),
            P(None, "row", None, "col"),
            P("col", None, "row"),
            P("col", None, "row"),
        ),
        check_vma=False,
    )
```

```python
import jax
import jax.numpy as jnp
from jax import lax
from jax.sharding import PartitionSpec as P

HIGH = lax.Precision.HIGHEST


def _steps(n):
    k = n.bit_length() - 1
    assert (1 << k) == n
    return k


def _partner(n, s):
    return [(i, i ^ (1 << s)) for i in range(n)]


def _bitrev(i, k):
    return int(format(i, f"0{k}b")[::-1], 2) if k else 0


def _halve(buf, axis, n, idx):
    return _halve_from(buf, axis, n, idx, 0)


def _halve_from(buf, axis, n, idx, first, side=None):
    for s in range(first, _steps(n)):
        bit = (idx >> s) & 1
        half = buf.shape[-1] // 2
        keep = lax.dynamic_slice_in_dim(buf, bit * half, half, axis=buf.ndim - 1)
        send = lax.dynamic_slice_in_dim(buf, (1 - bit) * half, half, axis=buf.ndim - 1)
        if side is not None and s == first + 1:
            send, side = lax.optimization_barrier((send, side))
        buf = keep + lax.ppermute(send, axis, _partner(n, s))
    if side is not None:
        return buf, side
    return buf


def _double(buf, axis, n, idx, order):
    for s in order:
        bit = (idx >> s) & 1
        recv = lax.ppermute(buf, axis, _partner(n, s))
        buf = jnp.where(
            bit == 0,
            jnp.concatenate([buf, recv], axis=-1),
            jnp.concatenate([recv, buf], axis=-1),
        )
    return buf


def _butterfly(x, axis, n):
    for s in range(_steps(n)):
        x = x + lax.ppermute(x, axis, _partner(n, s))
    return x


def shards(solution, residual, direction, gradient, left_factors, right_factors, ranks):
    left = left_factors[:, 0, 0]
    right = right_factors[:, 0, 0]
    rounds, tile, rank_max = left.shape
    rhs = direction.shape[1]
    t_local = residual.shape[3]
    n_col = tile // t_local
    n_row = tile // direction.shape[2]
    c = lax.axis_index("col")
    r = lax.axis_index("row")
    mask = (
        jnp.arange(rank_max, dtype=jnp.int32)[None, None, :] < ranks[:, 0, 0][:, None, None]
    ).astype(jnp.float32)
    g_local = jnp.sum(gradient * gradient, axis=(0, 2))
    coeffs = (
        jnp.einsum(
            "hn,anm->ahm",
            lax.all_gather(direction, "row", axis=2, tiled=True)[0],
            right,
            precision=HIGH,
        )
        * mask
    )
    partial_image = jnp.einsum("ahm,atm->aht", coeffs, left, precision=HIGH)
    payload = partial_image.reshape(rounds * rhs, tile)
    k_col = _steps(n_col)
    res_order = [2, 0, 1] + list(range(3, k_col)) if k_col >= 3 else list(range(k_col))
    extra = jnp.zeros((8, t_local), jnp.float32).at[0, :rhs].set(g_local)
    res = jnp.concatenate([residual[:, 0].reshape(rounds * rhs, t_local), extra], axis=0)
    res = _double(res, "col", n_col, c, res_order[:-1])
    res, payload = lax.optimization_barrier((res, payload))
    bit = (c >> 0) & 1
    half = payload.shape[-1] // 2
    keep = lax.dynamic_slice_in_dim(payload, bit * half, half, axis=1)
    send = lax.dynamic_slice_in_dim(payload, (1 - bit) * half, half, axis=1)
    got = lax.ppermute(send, "col", _partner(n_col, 0))
    res = _double(res, "col", n_col, c, res_order[-1:])
    res, got = lax.optimization_barrier((res, got))
    where = [sum(((d >> s) & 1) << i for i, s in enumerate(res_order)) for d in range(n_col)]
    gamma_col = jnp.sum(res[rounds * rhs].reshape(n_col, t_local)[:, :rhs], axis=0)
    residual_full = res[: rounds * rhs].reshape(rounds, rhs, n_col, t_local)[:, :, jnp.array(where)]
    residual_full = residual_full.reshape(rounds, rhs, tile)
    back_res = jnp.einsum("aht,atm->ahm", residual_full, left, precision=HIGH) * mask
    summed = _halve_from(keep + got, "col", n_col, c, 1, back_res)
    back_res = summed[1]
    summed = _double(summed[0], "col", n_col, c, reversed(range(k_col)))
    image_full = summed.reshape(rounds, rhs, tile)
    d_local = jnp.sum(image_full * image_full, axis=(0, 2))
    sums = _butterfly(jnp.stack([gamma_col, d_local]), "row", n_row)
    gamma = sums[0]
    delta = sums[1]
    alpha = gamma / delta
    solution_new = solution + alpha[None, :, None] * direction
    image_mine = lax.dynamic_slice_in_dim(image_full, c * t_local, t_local, axis=2)
    residual_new = residual - alpha[None, None, :, None] * image_mine[:, None]
    back_img = jnp.einsum("aht,atm->ahm", image_full, left, precision=HIGH) * mask
    back = back_res - alpha[None, :, None] * back_img
    partial_gradient = jnp.einsum("ahm,anm->hn", back, right, precision=HIGH)
    k_row = _steps(n_row)
    order = [_bitrev(p, k_row) for p in range(n_row)]
    blocks = partial_gradient.reshape(rhs, n_row, tile // n_row)[:, jnp.array(order)]
    gradient_new = _halve(blocks.reshape(rhs, tile), "row", n_row, r)[None]
    g_new = _butterfly(_butterfly(jnp.sum(gradient_new * gradient_new, axis=(0, 2)), "row", n_row), "col", n_col)
    beta = g_new / gamma
    direction_new = gradient_new + beta[None, :, None] * direction
    return (solution_new, residual_new, direction_new, gradient_new)


def solution(mesh):
    return jax.shard_map(
        shards,
        mesh=mesh,
        in_specs=(
            P("col", None, "row"),
            P(None, "row", None, "col"),
            P("col", None, "row"),
            P("col", None, "row"),
            P(None, "row", "col", None, None),
            P(None, "row", "col", None, None),
            P(None, "row", "col"),
        ),
        out_specs=(
            P("col", None, "row"),
            P(None, "row", None, "col"),
            P("col", None, "row"),
            P("col", None, "row"),
        ),
        check_vma=False,
    )
```

```python
import jax
import jax.numpy as jnp
from jax import lax
from jax.sharding import PartitionSpec as P

HIGH = lax.Precision.HIGHEST


def _steps(n):
    k = n.bit_length() - 1
    assert (1 << k) == n
    return k


def _partner(n, s):
    return [(i, i ^ (1 << s)) for i in range(n)]


def _bitrev(i, k):
    return int(format(i, f"0{k}b")[::-1], 2) if k else 0


def _halve(buf, axis, n, idx):
    return _halve_from(buf, axis, n, idx, 0)


def _halve_from(buf, axis, n, idx, first, side=None):
    for s in range(first, _steps(n)):
        bit = (idx >> s) & 1
        half = buf.shape[-1] // 2
        keep = lax.dynamic_slice_in_dim(buf, bit * half, half, axis=buf.ndim - 1)
        send = lax.dynamic_slice_in_dim(buf, (1 - bit) * half, half, axis=buf.ndim - 1)
        if side is not None and s == first + 1:
            send, side = lax.optimization_barrier((send, side))
        buf = keep + lax.ppermute(send, axis, _partner(n, s))
    if side is not None:
        return buf, side
    return buf


def _all_reduce_rest(buf, axis, n, idx, side):
    k = _steps(n)
    for s in range(1, k):
        bit = (idx >> s) & 1
        if s < k - 1:
            half = buf.shape[-1] // 2
            keep = lax.dynamic_slice_in_dim(buf, bit * half, half, axis=buf.ndim - 1)
            send = lax.dynamic_slice_in_dim(buf, (1 - bit) * half, half, axis=buf.ndim - 1)
        else:
            keep, send = buf, buf
        if s == 2:
            send, side = lax.optimization_barrier((send, side))
        buf = keep + lax.ppermute(send, axis, _partner(n, s))
    return _double(buf, axis, n, idx, reversed(range(k - 1))), side


def _double(buf, axis, n, idx, order):
    for s in order:
        bit = (idx >> s) & 1
        recv = lax.ppermute(buf, axis, _partner(n, s))
        buf = jnp.where(
            bit == 0,
            jnp.concatenate([buf, recv], axis=-1),
            jnp.concatenate([recv, buf], axis=-1),
        )
    return buf


def _butterfly(x, axis, n):
    for s in range(_steps(n)):
        x = x + lax.ppermute(x, axis, _partner(n, s))
    return x


def shards(solution, residual, direction, gradient, left_factors, right_factors, ranks):
    left = left_factors[:, 0, 0]
    right = right_factors[:, 0, 0]
    rounds, tile, rank_max = left.shape
    rhs = direction.shape[1]
    t_local = residual.shape[3]
    n_col = tile // t_local
    n_row = tile // direction.shape[2]
    c = lax.axis_index("col")
    r = lax.axis_index("row")
    mask = (
        jnp.arange(rank_max, dtype=jnp.int32)[None, None, :] < ranks[:, 0, 0][:, None, None]
    ).astype(jnp.float32)
    g_local = jnp.sum(gradient * gradient, axis=(0, 2))
    coeffs = (
        jnp.einsum(
            "hn,anm->ahm",
            lax.all_gather(direction, "row", axis=2, tiled=True)[0],
            right,
            precision=HIGH,
        )
        * mask
    )
    partial_image = jnp.einsum("ahm,atm->aht", coeffs, left, precision=HIGH)
    payload = partial_image.reshape(rounds * rhs, tile)
    k_col = _steps(n_col)
    res_order = [2, 0, 1] + list(range(3, k_col)) if k_col >= 3 else list(range(k_col))
    extra = jnp.zeros((8, t_local), jnp.float32).at[0, :rhs].set(g_local)
    res = jnp.concatenate([residual[:, 0].reshape(rounds * rhs, t_local), extra], axis=0)
    res = _double(res, "col", n_col, c, res_order[:-1])
    res, payload = lax.optimization_barrier((res, payload))
    if k_col > 1:
        bit = (c >> 0) & 1
        half = payload.shape[-1] // 2
        keep = lax.dynamic_slice_in_dim(payload, bit * half, half, axis=1)
        send = lax.dynamic_slice_in_dim(payload, (1 - bit) * half, half, axis=1)
    else:
        keep, send = payload, payload
    got = lax.ppermute(send, "col", _partner(n_col, 0))
    res = _double(res, "col", n_col, c, res_order[-1:])
    res, got = lax.optimization_barrier((res, got))
    where = [sum(((d >> s) & 1) << i for i, s in enumerate(res_order)) for d in range(n_col)]
    gamma_col = jnp.sum(res[rounds * rhs].reshape(n_col, t_local)[:, :rhs], axis=0)
    residual_full = res[: rounds * rhs].reshape(rounds, rhs, n_col, t_local)[:, :, jnp.array(where)]
    residual_full = residual_full.reshape(rounds, rhs, tile)
    back_res = jnp.einsum("aht,atm->ahm", residual_full, left, precision=HIGH) * mask
    summed, back_res = _all_reduce_rest(keep + got, "col", n_col, c, back_res)
    image_full = summed.reshape(rounds, rhs, tile)
    d_local = jnp.sum(image_full * image_full, axis=(0, 2))
    sums = _butterfly(jnp.stack([gamma_col, d_local]), "row", n_row)
    gamma = sums[0]
    delta = sums[1]
    alpha = gamma / delta
    solution_new = solution + alpha[None, :, None] * direction
    image_mine = lax.dynamic_slice_in_dim(image_full, c * t_local, t_local, axis=2)
    residual_new = residual - alpha[None, None, :, None] * image_mine[:, None]
    back_img = jnp.einsum("aht,atm->ahm", image_full, left, precision=HIGH) * mask
    back = back_res - alpha[None, :, None] * back_img
    partial_gradient = jnp.einsum("ahm,anm->hn", back, right, precision=HIGH)
    k_row = _steps(n_row)
    order = [_bitrev(p, k_row) for p in range(n_row)]
    blocks = partial_gradient.reshape(rhs, n_row, tile // n_row)[:, jnp.array(order)]
    gradient_new = _halve(blocks.reshape(rhs, tile), "row", n_row, r)[None]
    g_new = _butterfly(_butterfly(jnp.sum(gradient_new * gradient_new, axis=(0, 2)), "row", n_row), "col", n_col)
    beta = g_new / gamma
    direction_new = gradient_new + beta[None, :, None] * direction
    return (solution_new, residual_new, direction_new, gradient_new)


def solution(mesh):
    return jax.shard_map(
        shards,
        mesh=mesh,
        in_specs=(
            P("col", None, "row"),
            P(None, "row", None, "col"),
            P("col", None, "row"),
            P("col", None, "row"),
            P(None, "row", "col", None, None),
            P(None, "row", "col", None, None),
            P(None, "row", "col"),
        ),
        out_specs=(
            P("col", None, "row"),
            P(None, "row", None, "col"),
            P("col", None, "row"),
            P("col", None, "row"),
        ),
        check_vma=False,
    )
```

```python
import jax
import jax.numpy as jnp
from jax import lax
from jax.sharding import PartitionSpec as P

HIGH = lax.Precision.HIGHEST


def _steps(n):
    k = n.bit_length() - 1
    assert (1 << k) == n
    return k


def _partner(n, s):
    return [(i, i ^ (1 << s)) for i in range(n)]


def _bitrev(i, k):
    return int(format(i, f"0{k}b")[::-1], 2) if k else 0


def _halve(buf, axis, n, idx):
    return _halve_from(buf, axis, n, idx, 0)


def _halve_from(buf, axis, n, idx, first, side=None):
    for s in range(first, _steps(n)):
        bit = (idx >> s) & 1
        half = buf.shape[-1] // 2
        keep = lax.dynamic_slice_in_dim(buf, bit * half, half, axis=buf.ndim - 1)
        send = lax.dynamic_slice_in_dim(buf, (1 - bit) * half, half, axis=buf.ndim - 1)
        if side is not None and s == first + 1:
            send, side = lax.optimization_barrier((send, side))
        buf = keep + lax.ppermute(send, axis, _partner(n, s))
    if side is not None:
        return buf, side
    return buf


def _double(buf, axis, n, idx, order):
    for s in order:
        bit = (idx >> s) & 1
        recv = lax.ppermute(buf, axis, _partner(n, s))
        buf = jnp.where(
            bit == 0,
            jnp.concatenate([buf, recv], axis=-1),
            jnp.concatenate([recv, buf], axis=-1),
        )
    return buf


def _butterfly(x, axis, n):
    for s in range(_steps(n)):
        x = x + lax.ppermute(x, axis, _partner(n, s))
    return x


def shards(solution, residual, direction, gradient, left_factors, right_factors, ranks):
    left = left_factors[:, 0, 0]
    right = right_factors[:, 0, 0]
    rounds, tile, rank_max = left.shape
    rhs = direction.shape[1]
    t_local = residual.shape[3]
    n_col = tile // t_local
    n_row = tile // direction.shape[2]
    c = lax.axis_index("col")
    r = lax.axis_index("row")
    mask = (
        jnp.arange(rank_max, dtype=jnp.int32)[None, None, :] < ranks[:, 0, 0][:, None, None]
    ).astype(jnp.float32)
    g_local = jnp.sum(gradient * gradient, axis=(0, 2))
    coeffs = (
        jnp.einsum(
            "hn,anm->ahm",
            _double(direction[0], "row", n_row, r, range(_steps(n_row))),
            right,
            precision=HIGH,
        )
        * mask
    )
    partial_image = jnp.einsum("ahm,atm->aht", coeffs, left, precision=HIGH)
    payload = partial_image.reshape(rounds * rhs, tile)
    k_col = _steps(n_col)
    res_order = [2, 0, 1] + list(range(3, k_col)) if k_col >= 3 else list(range(k_col))
    extra = jnp.zeros((8, t_local), jnp.float32).at[0, :rhs].set(g_local)
    res = jnp.concatenate([residual[:, 0].reshape(rounds * rhs, t_local), extra], axis=0)
    res = _double(res, "col", n_col, c, res_order[:-1])
    res, payload = lax.optimization_barrier((res, payload))
    bit = (c >> 0) & 1
    half = payload.shape[-1] // 2
    keep = lax.dynamic_slice_in_dim(payload, bit * half, half, axis=1)
    send = lax.dynamic_slice_in_dim(payload, (1 - bit) * half, half, axis=1)
    got = lax.ppermute(send, "col", _partner(n_col, 0))
    res = _double(res, "col", n_col, c, res_order[-1:])
    res, got = lax.optimization_barrier((res, got))
    where = [sum(((d >> s) & 1) << i for i, s in enumerate(res_order)) for d in range(n_col)]
    gamma_col = jnp.sum(res[rounds * rhs].reshape(n_col, t_local)[:, :rhs], axis=0)
    residual_full = res[: rounds * rhs].reshape(rounds, rhs, n_col, t_local)[:, :, jnp.array(where)]
    residual_full = residual_full.reshape(rounds, rhs, tile)
    back_res = jnp.einsum("aht,atm->ahm", residual_full, left, precision=HIGH) * mask
    summed = _halve_from(keep + got, "col", n_col, c, 1, back_res)
    back_res = summed[1]
    summed = _double(summed[0], "col", n_col, c, reversed(range(k_col)))
    image_full = summed.reshape(rounds, rhs, tile)
    d_local = jnp.sum(image_full * image_full, axis=(0, 2))
    sums = _butterfly(jnp.stack([gamma_col, d_local]), "row", n_row)
    gamma = sums[0]
    delta = sums[1]
    alpha = gamma / delta
    solution_new = solution + alpha[None, :, None] * direction
    image_mine = lax.dynamic_slice_in_dim(image_full, c * t_local, t_local, axis=2)
    residual_new = residual - alpha[None, None, :, None] * image_mine[:, None]
    back_img = jnp.einsum("aht,atm->ahm", image_full, left, precision=HIGH) * mask
    back = back_res - alpha[None, :, None] * back_img
    partial_gradient = jnp.einsum("ahm,anm->hn", back, right, precision=HIGH)
    k_row = _steps(n_row)
    order = [_bitrev(p, k_row) for p in range(n_row)]
    blocks = partial_gradient.reshape(rhs, n_row, tile // n_row)[:, jnp.array(order)]
    gradient_new = _halve(blocks.reshape(rhs, tile), "row", n_row, r)[None]
    g_new = _butterfly(_butterfly(jnp.sum(gradient_new * gradient_new, axis=(0, 2)), "row", n_row), "col", n_col)
    beta = g_new / gamma
    direction_new = gradient_new + beta[None, :, None] * direction
    return (solution_new, residual_new, direction_new, gradient_new)


def solution(mesh):
    return jax.shard_map(
        shards,
        mesh=mesh,
        in_specs=(
            P("col", None, "row"),
            P(None, "row", None, "col"),
            P("col", None, "row"),
            P("col", None, "row"),
            P(None, "row", "col", None, None),
            P(None, "row", "col", None, None),
            P(None, "row", "col"),
        ),
        out_specs=(
            P("col", None, "row"),
            P(None, "row", None, "col"),
            P("col", None, "row"),
            P("col", None, "row"),
        ),
        check_vma=False,
    )
```

```python
import jax
import jax.numpy as jnp
from jax import lax
from jax.sharding import PartitionSpec as P

HIGH = lax.Precision.HIGH


def _steps(n):
    k = n.bit_length() - 1
    assert (1 << k) == n
    return k


def _partner(n, s):
    return [(i, i ^ (1 << s)) for i in range(n)]


def _bitrev(i, k):
    return int(format(i, f"0{k}b")[::-1], 2) if k else 0


def _halve(buf, axis, n, idx):
    return _halve_from(buf, axis, n, idx, 0)


def _halve_from(buf, axis, n, idx, first, side=None):
    for s in range(first, _steps(n)):
        bit = (idx >> s) & 1
        half = buf.shape[-1] // 2
        keep = lax.dynamic_slice_in_dim(buf, bit * half, half, axis=buf.ndim - 1)
        send = lax.dynamic_slice_in_dim(buf, (1 - bit) * half, half, axis=buf.ndim - 1)
        if side is not None and s == first + 1:
            send, side = lax.optimization_barrier((send, side))
        buf = keep + lax.ppermute(send, axis, _partner(n, s))
    if side is not None:
        return buf, side
    return buf


def _double(buf, axis, n, idx, order):
    for s in order:
        bit = (idx >> s) & 1
        recv = lax.ppermute(buf, axis, _partner(n, s))
        buf = jnp.where(
            bit == 0,
            jnp.concatenate([buf, recv], axis=-1),
            jnp.concatenate([recv, buf], axis=-1),
        )
    return buf


def _butterfly(x, axis, n):
    for s in range(_steps(n)):
        x = x + lax.ppermute(x, axis, _partner(n, s))
    return x


def shards(solution, residual, direction, gradient, left_factors, right_factors, ranks):
    left = left_factors[:, 0, 0]
    right = right_factors[:, 0, 0]
    rounds, tile, rank_max = left.shape
    rhs = direction.shape[1]
    t_local = residual.shape[3]
    n_col = tile // t_local
    n_row = tile // direction.shape[2]
    c = lax.axis_index("col")
    r = lax.axis_index("row")
    mask = (
        jnp.arange(rank_max, dtype=jnp.int32)[None, None, :] < ranks[:, 0, 0][:, None, None]
    ).astype(jnp.float32)
    g_local = jnp.sum(gradient * gradient, axis=(0, 2))
    coeffs = (
        jnp.einsum(
            "hn,anm->ahm",
            lax.all_gather(direction, "row", axis=2, tiled=True)[0],
            right,
            precision=HIGH,
        )
        * mask
    )
    partial_image = jnp.einsum("ahm,atm->aht", coeffs, left, precision=HIGH)
    payload = partial_image.reshape(rounds * rhs, tile)
    k_col = _steps(n_col)
    res_order = [2, 0, 1] + list(range(3, k_col)) if k_col >= 3 else list(range(k_col))
    extra = jnp.zeros((8, t_local), jnp.float32).at[0, :rhs].set(g_local)
    res = jnp.concatenate([residual[:, 0].reshape(rounds * rhs, t_local), extra], axis=0)
    res = _double(res, "col", n_col, c, res_order[:-1])
    res, payload = lax.optimization_barrier((res, payload))
    bit = (c >> 0) & 1
    half = payload.shape[-1] // 2
    keep = lax.dynamic_slice_in_dim(payload, bit * half, half, axis=1)
    send = lax.dynamic_slice_in_dim(payload, (1 - bit) * half, half, axis=1)
    got = lax.ppermute(send, "col", _partner(n_col, 0))
    res = _double(res, "col", n_col, c, res_order[-1:])
    res, got = lax.optimization_barrier((res, got))
    where = [sum(((d >> s) & 1) << i for i, s in enumerate(res_order)) for d in range(n_col)]
    gamma_col = jnp.sum(res[rounds * rhs].reshape(n_col, t_local)[:, :rhs], axis=0)
    residual_full = res[: rounds * rhs].reshape(rounds, rhs, n_col, t_local)[:, :, jnp.array(where)]
    residual_full = residual_full.reshape(rounds, rhs, tile)
    back_res = jnp.einsum("aht,atm->ahm", residual_full, left, precision=HIGH) * mask
    summed = _halve_from(keep + got, "col", n_col, c, 1, back_res)
    back_res = summed[1]
    summed = _double(summed[0], "col", n_col, c, reversed(range(k_col)))
    image_full = summed.reshape(rounds, rhs, tile)
    d_local = jnp.sum(image_full * image_full, axis=(0, 2))
    sums = _butterfly(jnp.stack([gamma_col, d_local]), "row", n_row)
    gamma = sums[0]
    delta = sums[1]
    alpha = gamma / delta
    solution_new = solution + alpha[None, :, None] * direction
    image_mine = lax.dynamic_slice_in_dim(image_full, c * t_local, t_local, axis=2)
    residual_new = residual - alpha[None, None, :, None] * image_mine[:, None]
    back_img = jnp.einsum("aht,atm->ahm", image_full, left, precision=HIGH) * mask
    back = back_res - alpha[None, :, None] * back_img
    partial_gradient = jnp.einsum("ahm,anm->hn", back, right, precision=HIGH)
    k_row = _steps(n_row)
    order = [_bitrev(p, k_row) for p in range(n_row)]
    blocks = partial_gradient.reshape(rhs, n_row, tile // n_row)[:, jnp.array(order)]
    gradient_new = _halve(blocks.reshape(rhs, tile), "row", n_row, r)[None]
    g_new = _butterfly(_butterfly(jnp.sum(gradient_new * gradient_new, axis=(0, 2)), "row", n_row), "col", n_col)
    beta = g_new / gamma
    direction_new = gradient_new + beta[None, :, None] * direction
    return (solution_new, residual_new, direction_new, gradient_new)


def solution(mesh):
    return jax.shard_map(
        shards,
        mesh=mesh,
        in_specs=(
            P("col", None, "row"),
            P(None, "row", None, "col"),
            P("col", None, "row"),
            P("col", None, "row"),
            P(None, "row", "col", None, None),
            P(None, "row", "col", None, None),
            P(None, "row", "col"),
        ),
        out_specs=(
            P("col", None, "row"),
            P(None, "row", None, "col"),
            P("col", None, "row"),
            P("col", None, "row"),
        ),
        check_vma=False,
    )
```

```python
import jax
import jax.numpy as jnp
from jax import lax
from jax.sharding import PartitionSpec as P

BF16 = jnp.bfloat16


def _split(x):
    hi = lax.reduce_precision(x, exponent_bits=8, mantissa_bits=7)
    return hi.astype(BF16), (x - hi).astype(BF16)


def _mm(eq, a, b):
    a_hi, a_lo = _split(a)
    b_hi, b_lo = b

    def one(x, y):
        return jnp.einsum(eq, x, y, preferred_element_type=jnp.float32)

    return one(a_hi, b_hi) + (one(a_hi, b_lo) + one(a_lo, b_hi))


def _steps(n):
    k = n.bit_length() - 1
    assert (1 << k) == n
    return k


def _partner(n, s):
    return [(i, i ^ (1 << s)) for i in range(n)]


def _bitrev(i, k):
    return int(format(i, f"0{k}b")[::-1], 2) if k else 0


def _halve(buf, axis, n, idx):
    return _halve_from(buf, axis, n, idx, 0)


def _halve_from(buf, axis, n, idx, first, side=None):
    for s in range(first, _steps(n)):
        bit = (idx >> s) & 1
        half = buf.shape[-1] // 2
        keep = lax.dynamic_slice_in_dim(buf, bit * half, half, axis=buf.ndim - 1)
        send = lax.dynamic_slice_in_dim(buf, (1 - bit) * half, half, axis=buf.ndim - 1)
        if side is not None and s == first + 1:
            send, side = lax.optimization_barrier((send, side))
        buf = keep + lax.ppermute(send, axis, _partner(n, s))
    if side is not None:
        return buf, side
    return buf


def _double(buf, axis, n, idx, order):
    for s in order:
        bit = (idx >> s) & 1
        recv = lax.ppermute(buf, axis, _partner(n, s))
        buf = jnp.where(
            bit == 0,
            jnp.concatenate([buf, recv], axis=-1),
            jnp.concatenate([recv, buf], axis=-1),
        )
    return buf


def _butterfly(x, axis, n):
    for s in range(_steps(n)):
        x = x + lax.ppermute(x, axis, _partner(n, s))
    return x


def shards(solution, residual, direction, gradient, left_factors, right_factors, ranks):
    rounds, tile, rank_max = left_factors[:, 0, 0].shape
    left = _split(left_factors[:, 0, 0])
    right = _split(right_factors[:, 0, 0])
    rhs = direction.shape[1]
    t_local = residual.shape[3]
    n_col = tile // t_local
    n_row = tile // direction.shape[2]
    c = lax.axis_index("col")
    r = lax.axis_index("row")
    mask = (
        jnp.arange(rank_max, dtype=jnp.int32)[None, None, :] < ranks[:, 0, 0][:, None, None]
    ).astype(jnp.float32)
    g_local = jnp.sum(gradient * gradient, axis=(0, 2))
    coeffs = (
        _mm("hn,anm->ahm", lax.all_gather(direction, "row", axis=2, tiled=True)[0], right)
        * mask
    )
    partial_image = _mm("ahm,atm->aht", coeffs, left)
    payload = partial_image.reshape(rounds * rhs, tile)
    k_col = _steps(n_col)
    res_order = [2, 0, 1] + list(range(3, k_col)) if k_col >= 3 else list(range(k_col))
    extra = jnp.zeros((8, t_local), jnp.float32).at[0, :rhs].set(g_local)
    res = jnp.concatenate([residual[:, 0].reshape(rounds * rhs, t_local), extra], axis=0)
    res = _double(res, "col", n_col, c, res_order[:-1])
    res, payload = lax.optimization_barrier((res, payload))
    bit = (c >> 0) & 1
    half = payload.shape[-1] // 2
    keep = lax.dynamic_slice_in_dim(payload, bit * half, half, axis=1)
    send = lax.dynamic_slice_in_dim(payload, (1 - bit) * half, half, axis=1)
    got = lax.ppermute(send, "col", _partner(n_col, 0))
    res = _double(res, "col", n_col, c, res_order[-1:])
    res, got = lax.optimization_barrier((res, got))
    where = [sum(((d >> s) & 1) << i for i, s in enumerate(res_order)) for d in range(n_col)]
    gamma_col = jnp.sum(res[rounds * rhs].reshape(n_col, t_local)[:, :rhs], axis=0)
    residual_full = res[: rounds * rhs].reshape(rounds, rhs, n_col, t_local)[:, :, jnp.array(where)]
    residual_full = residual_full.reshape(rounds, rhs, tile)
    back_res = _mm("aht,atm->ahm", residual_full, left) * mask
    summed = _halve_from(keep + got, "col", n_col, c, 1, back_res)
    back_res = summed[1]
    summed = _double(summed[0], "col", n_col, c, reversed(range(k_col)))
    image_full = summed.reshape(rounds, rhs, tile)
    d_local = jnp.sum(image_full * image_full, axis=(0, 2))
    sums = _butterfly(jnp.stack([gamma_col, d_local]), "row", n_row)
    gamma = sums[0]
    delta = sums[1]
    alpha = gamma / delta
    solution_new = solution + alpha[None, :, None] * direction
    image_mine = lax.dynamic_slice_in_dim(image_full, c * t_local, t_local, axis=2)
    residual_new = residual - alpha[None, None, :, None] * image_mine[:, None]
    back_img = _mm("aht,atm->ahm", image_full, left) * mask
    back = back_res - alpha[None, :, None] * back_img
    partial_gradient = _mm("ahm,anm->hn", back, right)
    k_row = _steps(n_row)
    order = [_bitrev(p, k_row) for p in range(n_row)]
    blocks = partial_gradient.reshape(rhs, n_row, tile // n_row)[:, jnp.array(order)]
    gradient_new = _halve(blocks.reshape(rhs, tile), "row", n_row, r)[None]
    g_new = _butterfly(_butterfly(jnp.sum(gradient_new * gradient_new, axis=(0, 2)), "row", n_row), "col", n_col)
    beta = g_new / gamma
    direction_new = gradient_new + beta[None, :, None] * direction
    return (solution_new, residual_new, direction_new, gradient_new)


def solution(mesh):
    return jax.shard_map(
        shards,
        mesh=mesh,
        in_specs=(
            P("col", None, "row"),
            P(None, "row", None, "col"),
            P("col", None, "row"),
            P("col", None, "row"),
            P(None, "row", "col", None, None),
            P(None, "row", "col", None, None),
            P(None, "row", "col"),
        ),
        out_specs=(
            P("col", None, "row"),
            P(None, "row", None, "col"),
            P("col", None, "row"),
            P("col", None, "row"),
        ),
        check_vma=False,
    )
```

```python
import jax
import jax.numpy as jnp
from jax import lax
from jax.sharding import PartitionSpec as P

HIGH = lax.Precision.HIGH


def _steps(n):
    k = n.bit_length() - 1
    assert (1 << k) == n
    return k


def _partner(n, s):
    return [(i, i ^ (1 << s)) for i in range(n)]


def _bitrev(i, k):
    return int(format(i, f"0{k}b")[::-1], 2) if k else 0


def _halve(buf, axis, n, idx):
    return _halve_from(buf, axis, n, idx, 0)


def _halve_from(buf, axis, n, idx, first, side=None):
    for s in range(first, _steps(n)):
        bit = (idx >> s) & 1
        half = buf.shape[-1] // 2
        keep = lax.dynamic_slice_in_dim(buf, bit * half, half, axis=buf.ndim - 1)
        send = lax.dynamic_slice_in_dim(buf, (1 - bit) * half, half, axis=buf.ndim - 1)
        if side is not None and s == first + 1:
            send, side = lax.optimization_barrier((send, side))
        buf = keep + lax.ppermute(send, axis, _partner(n, s))
    if side is not None:
        return buf, side
    return buf


def _double(buf, axis, n, idx, order, side=None):
    for i, s in enumerate(order):
        bit = (idx >> s) & 1
        if side is not None and i == 1:
            buf, side = lax.optimization_barrier((buf, side))
        recv = lax.ppermute(buf, axis, _partner(n, s))
        buf = jnp.where(
            bit == 0,
            jnp.concatenate([buf, recv], axis=-1),
            jnp.concatenate([recv, buf], axis=-1),
        )
    if side is not None:
        return buf, side
    return buf


def _butterfly(x, axis, n):
    for s in range(_steps(n)):
        x = x + lax.ppermute(x, axis, _partner(n, s))
    return x


def shards(solution, residual, direction, gradient, left_factors, right_factors, ranks):
    left = left_factors[:, 0, 0]
    right = right_factors[:, 0, 0]
    rounds, tile, rank_max = left.shape
    rhs = direction.shape[1]
    t_local = residual.shape[3]
    n_col = tile // t_local
    n_row = tile // direction.shape[2]
    c = lax.axis_index("col")
    r = lax.axis_index("row")
    mask = (
        jnp.arange(rank_max, dtype=jnp.int32)[None, None, :] < ranks[:, 0, 0][:, None, None]
    ).astype(jnp.float32)
    g_local = jnp.sum(gradient * gradient, axis=(0, 2))
    coeffs = (
        jnp.einsum(
            "hn,anm->ahm",
            lax.all_gather(direction, "row", axis=2, tiled=True)[0],
            right,
            precision=HIGH,
        )
        * mask
    )
    partial_image = jnp.einsum("ahm,atm->aht", coeffs, left, precision=HIGH)
    payload = partial_image.reshape(rounds * rhs, tile)
    k_col = _steps(n_col)
    res_order = [2, 0, 1] + list(range(3, k_col)) if k_col >= 3 else list(range(k_col))
    extra = jnp.zeros((8, t_local), jnp.float32).at[0, :rhs].set(g_local)
    res = jnp.concatenate([residual[:, 0].reshape(rounds * rhs, t_local), extra], axis=0)
    res = _double(res, "col", n_col, c, res_order[:-1])
    res, payload = lax.optimization_barrier((res, payload))
    bit = (c >> 0) & 1
    half = payload.shape[-1] // 2
    keep = lax.dynamic_slice_in_dim(payload, bit * half, half, axis=1)
    send = lax.dynamic_slice_in_dim(payload, (1 - bit) * half, half, axis=1)
    got = lax.ppermute(send, "col", _partner(n_col, 0))
    res = _double(res, "col", n_col, c, res_order[-1:])
    res, got = lax.optimization_barrier((res, got))
    where = [sum(((d >> s) & 1) << i for i, s in enumerate(res_order)) for d in range(n_col)]
    gamma_col = jnp.sum(res[rounds * rhs].reshape(n_col, t_local)[:, :rhs], axis=0)
    residual_full = res[: rounds * rhs].reshape(rounds, rhs, n_col, t_local)[:, :, jnp.array(where)]
    residual_full = residual_full.reshape(rounds, rhs, tile)
    back_res = jnp.einsum("aht,atm->ahm", residual_full, left, precision=HIGH) * mask
    summed = _halve_from(keep + got, "col", n_col, c, 1, back_res)
    back_res = summed[1]
    p_res = jnp.einsum("ahm,anm->hn", back_res, right, precision=HIGH)
    summed, p_res = _double(summed[0], "col", n_col, c, list(reversed(range(k_col))), p_res)
    image_full = summed.reshape(rounds, rhs, tile)
    d_local = jnp.sum(image_full * image_full, axis=(0, 2))
    sums = _butterfly(jnp.stack([gamma_col, d_local]), "row", n_row)
    gamma = sums[0]
    delta = sums[1]
    alpha = gamma / delta
    solution_new = solution + alpha[None, :, None] * direction
    image_mine = lax.dynamic_slice_in_dim(image_full, c * t_local, t_local, axis=2)
    residual_new = residual - alpha[None, None, :, None] * image_mine[:, None]
    back_img = jnp.einsum("aht,atm->ahm", image_full, left, precision=HIGH) * mask
    p_img = jnp.einsum("ahm,anm->hn", back_img, right, precision=HIGH)
    partial_gradient = p_res - alpha[:, None] * p_img
    k_row = _steps(n_row)
    order = [_bitrev(p, k_row) for p in range(n_row)]
    blocks = partial_gradient.reshape(rhs, n_row, tile // n_row)[:, jnp.array(order)]
    gradient_new = _halve(blocks.reshape(rhs, tile), "row", n_row, r)[None]
    g_new = _butterfly(_butterfly(jnp.sum(gradient_new * gradient_new, axis=(0, 2)), "row", n_row), "col", n_col)
    beta = g_new / gamma
    direction_new = gradient_new + beta[None, :, None] * direction
    return (solution_new, residual_new, direction_new, gradient_new)


def solution(mesh):
    return jax.shard_map(
        shards,
        mesh=mesh,
        in_specs=(
            P("col", None, "row"),
            P(None, "row", None, "col"),
            P("col", None, "row"),
            P("col", None, "row"),
            P(None, "row", "col", None, None),
            P(None, "row", "col", None, None),
            P(None, "row", "col"),
        ),
        out_specs=(
            P("col", None, "row"),
            P(None, "row", None, "col"),
            P("col", None, "row"),
            P("col", None, "row"),
        ),
        check_vma=False,
    )
```

```python
import jax
import jax.numpy as jnp
from jax import lax
from jax.sharding import PartitionSpec as P

HIGH = lax.Precision.HIGH


def _steps(n):
    k = n.bit_length() - 1
    assert (1 << k) == n
    return k


def _partner(n, s):
    return [(i, i ^ (1 << s)) for i in range(n)]


def _bitrev(i, k):
    return int(format(i, f"0{k}b")[::-1], 2) if k else 0


def _halve(buf, axis, n, idx):
    return _halve_from(buf, axis, n, idx, 0)


def _halve_from(buf, axis, n, idx, first, side=None):
    for s in range(first, _steps(n)):
        bit = (idx >> s) & 1
        half = buf.shape[-1] // 2
        keep = lax.dynamic_slice_in_dim(buf, bit * half, half, axis=buf.ndim - 1)
        send = lax.dynamic_slice_in_dim(buf, (1 - bit) * half, half, axis=buf.ndim - 1)
        if side is not None and s == first + 1:
            send, side = lax.optimization_barrier((send, side))
        buf = keep + lax.ppermute(send, axis, _partner(n, s))
    if side is not None:
        return buf, side
    return buf


def _double(buf, axis, n, idx, order, side=None):
    for i, s in enumerate(order):
        bit = (idx >> s) & 1
        if side is not None and i == 1:
            buf, side = lax.optimization_barrier((buf, side))
        recv = lax.ppermute(buf, axis, _partner(n, s))
        buf = jnp.where(
            bit == 0,
            jnp.concatenate([buf, recv], axis=-1),
            jnp.concatenate([recv, buf], axis=-1),
        )
    if side is not None:
        return buf, side
    return buf


def _butterfly(x, axis, n):
    for s in range(_steps(n)):
        x = x + lax.ppermute(x, axis, _partner(n, s))
    return x


def shards(solution, residual, direction, gradient, left_factors, right_factors, ranks):
    left = left_factors[:, 0, 0]
    right = right_factors[:, 0, 0]
    rounds, tile, rank_max = left.shape
    rhs = direction.shape[1]
    t_local = residual.shape[3]
    n_col = tile // t_local
    n_row = tile // direction.shape[2]
    c = lax.axis_index("col")
    r = lax.axis_index("row")
    mask = (
        jnp.arange(rank_max, dtype=jnp.int32)[None, None, :] < ranks[:, 0, 0][:, None, None]
    ).astype(jnp.float32)
    g_local = jnp.sum(gradient * gradient, axis=(0, 2))
    coeffs = (
        jnp.einsum(
            "hn,anm->ahm",
            lax.all_gather(direction, "row", axis=2, tiled=True)[0],
            right,
            precision=HIGH,
        )
        * mask
    )

    def image_part(start, size):
        rows = lax.dynamic_slice_in_dim(left, start, size, axis=1)
        part = jnp.einsum("ahm,atm->aht", coeffs, rows, precision=HIGH)
        return part.reshape(rounds * rhs, size)

    k_col = _steps(n_col)
    res_order = [2, 0, 1] + list(range(3, k_col)) if k_col >= 3 else list(range(k_col))
    extra = jnp.zeros((8, t_local), jnp.float32).at[0, :rhs].set(g_local)
    res = jnp.concatenate([residual[:, 0].reshape(rounds * rhs, t_local), extra], axis=0)
    res = _double(res, "col", n_col, c, res_order[:-1])
    bit = (c >> 0) & 1
    half = tile // 2
    send = image_part((1 - bit) * half, half)
    res, send = lax.optimization_barrier((res, send))
    keep = image_part(bit * half, half)
    got = lax.ppermute(send, "col", _partner(n_col, 0))
    res = _double(res, "col", n_col, c, res_order[-1:])
    res, got = lax.optimization_barrier((res, got))
    where = [sum(((d >> s) & 1) << i for i, s in enumerate(res_order)) for d in range(n_col)]
    gamma_col = jnp.sum(res[rounds * rhs].reshape(n_col, t_local)[:, :rhs], axis=0)
    residual_full = res[: rounds * rhs].reshape(rounds, rhs, n_col, t_local)[:, :, jnp.array(where)]
    residual_full = residual_full.reshape(rounds, rhs, tile)
    back_res = jnp.einsum("aht,atm->ahm", residual_full, left, precision=HIGH) * mask
    summed = _halve_from(keep + got, "col", n_col, c, 1, back_res)
    back_res = summed[1]
    p_res = jnp.einsum("ahm,anm->hn", back_res, right, precision=HIGH)
    summed, p_res = _double(summed[0], "col", n_col, c, list(reversed(range(k_col))), p_res)
    image_full = summed.reshape(rounds, rhs, tile)
    d_local = jnp.sum(image_full * image_full, axis=(0, 2))
    sums = _butterfly(jnp.stack([gamma_col, d_local]), "row", n_row)
    gamma = sums[0]
    delta = sums[1]
    alpha = gamma / delta
    solution_new = solution + alpha[None, :, None] * direction
    image_mine = lax.dynamic_slice_in_dim(image_full, c * t_local, t_local, axis=2)
    residual_new = residual - alpha[None, None, :, None] * image_mine[:, None]
    back_img = jnp.einsum("aht,atm->ahm", image_full, left, precision=HIGH) * mask
    p_img = jnp.einsum("ahm,anm->hn", back_img, right, precision=HIGH)
    partial_gradient = p_res - alpha[:, None] * p_img
    k_row = _steps(n_row)
    order = [_bitrev(p, k_row) for p in range(n_row)]
    blocks = partial_gradient.reshape(rhs, n_row, tile // n_row)[:, jnp.array(order)]
    gradient_new = _halve(blocks.reshape(rhs, tile), "row", n_row, r)[None]
    g_new = _butterfly(_butterfly(jnp.sum(gradient_new * gradient_new, axis=(0, 2)), "row", n_row), "col", n_col)
    beta = g_new / gamma
    direction_new = gradient_new + beta[None, :, None] * direction
    return (solution_new, residual_new, direction_new, gradient_new)


def solution(mesh):
    return jax.shard_map(
        shards,
        mesh=mesh,
        in_specs=(
            P("col", None, "row"),
            P(None, "row", None, "col"),
            P("col", None, "row"),
            P("col", None, "row"),
            P(None, "row", "col", None, None),
            P(None, "row", "col", None, None),
            P(None, "row", "col"),
        ),
        out_specs=(
            P("col", None, "row"),
            P(None, "row", None, "col"),
            P("col", None, "row"),
            P("col", None, "row"),
        ),
        check_vma=False,
    )
```

```python
import jax
import jax.numpy as jnp
from jax import lax
from jax.sharding import PartitionSpec as P

HIGH = lax.Precision.HIGH


def _steps(n):
    k = n.bit_length() - 1
    assert (1 << k) == n
    return k


def _partner(n, s):
    return [(i, i ^ (1 << s)) for i in range(n)]


def _bitrev(i, k):
    return int(format(i, f"0{k}b")[::-1], 2) if k else 0


def _halve(buf, axis, n, idx):
    return _halve_from(buf, axis, n, idx, 0)


def _halve_from(buf, axis, n, idx, first, side=None):
    for s in range(first, _steps(n)):
        bit = (idx >> s) & 1
        half = buf.shape[-1] // 2
        keep = lax.dynamic_slice_in_dim(buf, bit * half, half, axis=buf.ndim - 1)
        send = lax.dynamic_slice_in_dim(buf, (1 - bit) * half, half, axis=buf.ndim - 1)
        if side is not None and s == first + 1:
            send, side = lax.optimization_barrier((send, side))
        buf = keep + lax.ppermute(send, axis, _partner(n, s))
    if side is not None:
        return buf, side
    return buf


def _join_lanes(bit, mine, theirs):
    return jnp.where(
        bit == 0,
        jnp.concatenate([mine, theirs], axis=-1),
        jnp.concatenate([theirs, mine], axis=-1),
    )


def _double(buf, axis, n, idx, order, side=None):
    for i, s in enumerate(order):
        bit = (idx >> s) & 1
        if side is not None and i == 1:
            buf, side = lax.optimization_barrier((buf, side))
        recv = lax.ppermute(buf, axis, _partner(n, s))
        buf = jnp.where(
            bit == 0,
            jnp.concatenate([buf, recv], axis=-1),
            jnp.concatenate([recv, buf], axis=-1),
        )
    if side is not None:
        return buf, side
    return buf


def _pair_perm(n_row, n_col, bits):
    return [
        (r * n_col + c, r * n_col + (c ^ (1 << bits[r & 1])))
        for r in range(n_row)
        for c in range(n_col)
    ]


def _pair_bit(c, odd, bits):
    return (c >> jnp.where(odd == 0, bits[0], bits[1])) & 1


def _butterfly(x, axis, n):
    for s in range(_steps(n)):
        x = x + lax.ppermute(x, axis, _partner(n, s))
    return x


def shards(solution, residual, direction, gradient, left_factors, right_factors, ranks):
    left = left_factors[:, 0, 0]
    right = right_factors[:, 0, 0]
    rounds, tile, rank_max = left.shape
    rhs = direction.shape[1]
    t_local = residual.shape[3]
    n_col = tile // t_local
    n_row = tile // direction.shape[2]
    c = lax.axis_index("col")
    r = lax.axis_index("row")
    mask = (
        jnp.arange(rank_max, dtype=jnp.int32)[None, None, :] < ranks[:, 0, 0][:, None, None]
    ).astype(jnp.float32)
    g_local = jnp.sum(gradient * gradient, axis=(0, 2))
    coeffs = (
        jnp.einsum(
            "hn,anm->ahm",
            lax.all_gather(direction, "row", axis=2, tiled=True)[0],
            right,
            precision=HIGH,
        )
        * mask
    )

    def image_part(start, size):
        rows = lax.dynamic_slice_in_dim(left, start, size, axis=1)
        part = jnp.einsum("ahm,atm->aht", coeffs, rows, precision=HIGH)
        return part.reshape(rounds * rhs, size)

    k_col = _steps(n_col)
    grid = ("row", "col")
    odd = r & 1
    if k_col >= 3:
        ar_order = ([0, 1] + list(range(2, k_col)), [1, 0] + list(range(2, k_col)))
        res_order = ([2, 0, 1] + list(range(3, k_col)), [2, 1, 0] + list(range(3, k_col)))
    else:
        ar_order = (list(range(k_col)), list(range(k_col)))
        res_order = ar_order

    def steps(order, i):
        return (order[0][i], order[1][i])

    def doubling(buf, i_steps, order):
        for i in i_steps:
            bits = steps(order, i)
            recv = lax.ppermute(buf, grid, _pair_perm(n_row, n_col, bits))
            buf = _join_lanes(_pair_bit(c, odd, bits), buf, recv)
        return buf

    extra = jnp.zeros((8, t_local), jnp.float32).at[0, :rhs].set(g_local)
    res = jnp.concatenate([residual[:, 0].reshape(rounds * rhs, t_local), extra], axis=0)
    res = doubling(res, range(k_col - 1), res_order)
    bits0 = steps(ar_order, 0)
    bit = _pair_bit(c, odd, bits0)
    half = tile // 2
    send = image_part((1 - bit) * half, half)
    res, send = lax.optimization_barrier((res, send))
    keep = image_part(bit * half, half)
    got = lax.ppermute(send, grid, _pair_perm(n_row, n_col, bits0))
    res = doubling(res, range(k_col - 1, k_col), res_order)
    res, got = lax.optimization_barrier((res, got))
    gamma_col = jnp.sum(res[rounds * rhs].reshape(n_col, t_local)[:, :rhs], axis=0)
    blocks_res = res[: rounds * rhs].reshape(rounds, rhs, n_col, t_local)
    placed = []
    for order in res_order:
        where = [sum(((d >> s) & 1) << i for i, s in enumerate(order)) for d in range(n_col)]
        placed.append(blocks_res[:, :, jnp.array(where)])
    residual_full = jnp.where(odd == 0, placed[0], placed[1]).reshape(rounds, rhs, tile)
    back_res = jnp.einsum("aht,atm->ahm", residual_full, left, precision=HIGH) * mask
    buf = keep + got
    for i in range(1, k_col):
        bits = steps(ar_order, i)
        bit = _pair_bit(c, odd, bits)
        half = buf.shape[-1] // 2
        keep = lax.dynamic_slice_in_dim(buf, bit * half, half, axis=1)
        send = lax.dynamic_slice_in_dim(buf, (1 - bit) * half, half, axis=1)
        if i == 2:
            send, back_res = lax.optimization_barrier((send, back_res))
        buf = keep + lax.ppermute(send, grid, _pair_perm(n_row, n_col, bits))
    p_res = jnp.einsum("ahm,anm->hn", back_res, right, precision=HIGH)
    for j, i in enumerate(reversed(range(k_col))):
        bits = steps(ar_order, i)
        if j == 1:
            buf, p_res = lax.optimization_barrier((buf, p_res))
        recv = lax.ppermute(buf, grid, _pair_perm(n_row, n_col, bits))
        buf = _join_lanes(_pair_bit(c, odd, bits), buf, recv)
    summed = buf
    image_full = summed.reshape(rounds, rhs, tile)
    d_local = jnp.sum(image_full * image_full, axis=(0, 2))
    sums = _butterfly(jnp.stack([gamma_col, d_local]), "row", n_row)
    gamma = sums[0]
    delta = sums[1]
    alpha = gamma / delta
    solution_new = solution + alpha[None, :, None] * direction
    image_mine = lax.dynamic_slice_in_dim(image_full, c * t_local, t_local, axis=2)
    residual_new = residual - alpha[None, None, :, None] * image_mine[:, None]
    back_img = jnp.einsum("aht,atm->ahm", image_full, left, precision=HIGH) * mask
    p_img = jnp.einsum("ahm,anm->hn", back_img, right, precision=HIGH)
    partial_gradient = p_res - alpha[:, None] * p_img
    k_row = _steps(n_row)
    order = [_bitrev(p, k_row) for p in range(n_row)]
    blocks = partial_gradient.reshape(rhs, n_row, tile // n_row)[:, jnp.array(order)]
    gradient_new = _halve(blocks.reshape(rhs, tile), "row", n_row, r)[None]
    g_new = _butterfly(_butterfly(jnp.sum(gradient_new * gradient_new, axis=(0, 2)), "row", n_row), "col", n_col)
    beta = g_new / gamma
    direction_new = gradient_new + beta[None, :, None] * direction
    return (solution_new, residual_new, direction_new, gradient_new)


def solution(mesh):
    return jax.shard_map(
        shards,
        mesh=mesh,
        in_specs=(
            P("col", None, "row"),
            P(None, "row", None, "col"),
            P("col", None, "row"),
            P("col", None, "row"),
            P(None, "row", "col", None, None),
            P(None, "row", "col", None, None),
            P(None, "row", "col"),
        ),
        out_specs=(
            P("col", None, "row"),
            P(None, "row", None, "col"),
            P("col", None, "row"),
            P("col", None, "row"),
        ),
        check_vma=False,
    )
```

```python
import jax
import jax.numpy as jnp
from jax import lax
from jax.sharding import PartitionSpec as P

HIGH = lax.Precision.HIGH


def _steps(n):
    k = n.bit_length() - 1
    assert (1 << k) == n
    return k


def _partner(n, s):
    return [(i, i ^ (1 << s)) for i in range(n)]


def _bitrev(i, k):
    return int(format(i, f"0{k}b")[::-1], 2) if k else 0


def _halve(buf, axis, n, idx):
    return _halve_from(buf, axis, n, idx, 0)


def _halve_from(buf, axis, n, idx, first, side=None):
    for s in range(first, _steps(n)):
        bit = (idx >> s) & 1
        half = buf.shape[-1] // 2
        keep = lax.dynamic_slice_in_dim(buf, bit * half, half, axis=buf.ndim - 1)
        send = lax.dynamic_slice_in_dim(buf, (1 - bit) * half, half, axis=buf.ndim - 1)
        if side is not None and s == first + 1:
            send, side = lax.optimization_barrier((send, side))
        buf = keep + lax.ppermute(send, axis, _partner(n, s))
    if side is not None:
        return buf, side
    return buf


def _join_lanes(bit, mine, theirs):
    return jnp.where(
        bit == 0,
        jnp.concatenate([mine, theirs], axis=-1),
        jnp.concatenate([theirs, mine], axis=-1),
    )


def _double(buf, axis, n, idx, order, side=None):
    for i, s in enumerate(order):
        bit = (idx >> s) & 1
        if side is not None and i == 1:
            buf, side = lax.optimization_barrier((buf, side))
        recv = lax.ppermute(buf, axis, _partner(n, s))
        buf = jnp.where(
            bit == 0,
            jnp.concatenate([buf, recv], axis=-1),
            jnp.concatenate([recv, buf], axis=-1),
        )
    if side is not None:
        return buf, side
    return buf


def _pair_perm(n_row, n_col, bits):
    return [
        (r * n_col + c, r * n_col + (c ^ (1 << bits[r & 1])))
        for r in range(n_row)
        for c in range(n_col)
    ]


def _pair_bit(c, odd, bits):
    return (c >> jnp.where(odd == 0, bits[0], bits[1])) & 1


def _butterfly(x, axis, n):
    for s in range(_steps(n)):
        x = x + lax.ppermute(x, axis, _partner(n, s))
    return x


def shards(solution, residual, direction, gradient, left_factors, right_factors, ranks):
    left = left_factors[:, 0, 0]
    right = right_factors[:, 0, 0]
    rounds, tile, rank_max = left.shape
    rhs = direction.shape[1]
    t_local = residual.shape[3]
    n_col = tile // t_local
    n_row = tile // direction.shape[2]
    c = lax.axis_index("col")
    r = lax.axis_index("row")
    mask = (
        jnp.arange(rank_max, dtype=jnp.int32)[None, None, :] < ranks[:, 0, 0][:, None, None]
    ).astype(jnp.float32)
    g_local = jnp.sum(gradient * gradient, axis=(0, 2))
    coeffs = (
        jnp.einsum(
            "hn,anm->ahm",
            lax.all_gather(direction, "row", axis=2, tiled=True)[0],
            right,
            precision=HIGH,
        )
        * mask
    )

    def image_part(start, size):
        rows = lax.dynamic_slice_in_dim(left, start, size, axis=1)
        part = jnp.einsum("ahm,atm->aht", coeffs, rows, precision=HIGH)
        return part.reshape(rounds * rhs, size)

    k_col = _steps(n_col)
    grid = ("row", "col")
    odd = r & 1
    if k_col >= 3:
        ar_order = ([0, 1] + list(range(2, k_col)), [1, 0] + list(range(2, k_col)))
        res_order = ([2, 0, 1] + list(range(3, k_col)), [2, 1, 0] + list(range(3, k_col)))
    else:
        ar_order = (list(range(k_col)), list(range(k_col)))
        res_order = ar_order

    def steps(order, i):
        return (order[0][i], order[1][i])

    def doubling(buf, i_steps, order):
        for i in i_steps:
            bits = steps(order, i)
            recv = lax.ppermute(buf, grid, _pair_perm(n_row, n_col, bits))
            buf = _join_lanes(_pair_bit(c, odd, bits), buf, recv)
        return buf

    extra = jnp.zeros((8, t_local), jnp.float32).at[0, :rhs].set(g_local)
    res = jnp.concatenate([residual[:, 0].reshape(rounds * rhs, t_local), extra], axis=0)
    res = doubling(res, range(k_col - 1), res_order)
    bits0 = steps(ar_order, 0)
    bit = _pair_bit(c, odd, bits0)
    half = tile // 2
    send = image_part((1 - bit) * half, half)
    res, send = lax.optimization_barrier((res, send))
    keep = image_part(bit * half, half)
    got = lax.ppermute(send, grid, _pair_perm(n_row, n_col, bits0))
    res = doubling(res, range(k_col - 1, k_col), res_order)
    res, got = lax.optimization_barrier((res, got))
    gamma_col = jnp.sum(res[rounds * rhs].reshape(n_col, t_local)[:, :rhs], axis=0)
    blocks_res = res[: rounds * rhs].reshape(rounds, rhs, n_col, t_local)
    placed = []
    for order in res_order:
        where = [sum(((d >> s) & 1) << i for i, s in enumerate(order)) for d in range(n_col)]
        placed.append(blocks_res[:, :, jnp.array(where)])
    residual_full = jnp.where(odd == 0, placed[0], placed[1]).reshape(rounds, rhs, tile)
    back_res = jnp.einsum("aht,atm->ahm", residual_full, left, precision=HIGH) * mask
    buf = keep + got
    for i in range(1, k_col):
        bits = steps(ar_order, i)
        bit = _pair_bit(c, odd, bits)
        half = buf.shape[-1] // 2
        keep = lax.dynamic_slice_in_dim(buf, bit * half, half, axis=1)
        send = lax.dynamic_slice_in_dim(buf, (1 - bit) * half, half, axis=1)
        buf = keep + lax.ppermute(send, grid, _pair_perm(n_row, n_col, bits))
    buf, back_res = lax.optimization_barrier((buf, back_res))
    p_res = jnp.einsum("ahm,anm->hn", back_res, right, precision=HIGH)
    for j, i in enumerate(reversed(range(k_col))):
        bits = steps(ar_order, i)
        if j == min(2, k_col - 1):
            buf, p_res = lax.optimization_barrier((buf, p_res))
        recv = lax.ppermute(buf, grid, _pair_perm(n_row, n_col, bits))
        buf = _join_lanes(_pair_bit(c, odd, bits), buf, recv)
    summed = buf
    image_full = summed.reshape(rounds, rhs, tile)
    d_local = jnp.sum(image_full * image_full, axis=(0, 2))
    sums = _butterfly(jnp.stack([gamma_col, d_local]), "row", n_row)
    gamma = sums[0]
    delta = sums[1]
    alpha = gamma / delta
    solution_new = solution + alpha[None, :, None] * direction
    image_mine = lax.dynamic_slice_in_dim(image_full, c * t_local, t_local, axis=2)
    residual_new = residual - alpha[None, None, :, None] * image_mine[:, None]
    back_img = jnp.einsum("aht,atm->ahm", image_full, left, precision=HIGH) * mask
    p_img = jnp.einsum("ahm,anm->hn", back_img, right, precision=HIGH)
    partial_gradient = p_res - alpha[:, None] * p_img
    k_row = _steps(n_row)
    order = [_bitrev(p, k_row) for p in range(n_row)]
    blocks = partial_gradient.reshape(rhs, n_row, tile // n_row)[:, jnp.array(order)]
    gradient_new = _halve(blocks.reshape(rhs, tile), "row", n_row, r)[None]
    g_new = _butterfly(_butterfly(jnp.sum(gradient_new * gradient_new, axis=(0, 2)), "row", n_row), "col", n_col)
    beta = g_new / gamma
    direction_new = gradient_new + beta[None, :, None] * direction
    return (solution_new, residual_new, direction_new, gradient_new)


def solution(mesh):
    return jax.shard_map(
        shards,
        mesh=mesh,
        in_specs=(
            P("col", None, "row"),
            P(None, "row", None, "col"),
            P("col", None, "row"),
            P("col", None, "row"),
            P(None, "row", "col", None, None),
            P(None, "row", "col", None, None),
            P(None, "row", "col"),
        ),
        out_specs=(
            P("col", None, "row"),
            P(None, "row", None, "col"),
            P("col", None, "row"),
            P("col", None, "row"),
        ),
        check_vma=False,
    )
```

```python
import jax
import jax.numpy as jnp
from jax import lax
from jax.sharding import PartitionSpec as P

HIGH = lax.Precision.HIGH


def _steps(n):
    k = n.bit_length() - 1
    assert (1 << k) == n
    return k


def _partner(n, s):
    return [(i, i ^ (1 << s)) for i in range(n)]


def _bitrev(i, k):
    return int(format(i, f"0{k}b")[::-1], 2) if k else 0


def _halve(buf, axis, n, idx):
    return _halve_from(buf, axis, n, idx, 0)


def _halve_from(buf, axis, n, idx, first, side=None):
    for s in range(first, _steps(n)):
        bit = (idx >> s) & 1
        half = buf.shape[-1] // 2
        keep = lax.dynamic_slice_in_dim(buf, bit * half, half, axis=buf.ndim - 1)
        send = lax.dynamic_slice_in_dim(buf, (1 - bit) * half, half, axis=buf.ndim - 1)
        if side is not None and s == first + 1:
            send, side = lax.optimization_barrier((send, side))
        buf = keep + lax.ppermute(send, axis, _partner(n, s))
    if side is not None:
        return buf, side
    return buf


def _join_lanes(bit, mine, theirs):
    return jnp.where(
        bit == 0,
        jnp.concatenate([mine, theirs], axis=-1),
        jnp.concatenate([theirs, mine], axis=-1),
    )


def _double(buf, axis, n, idx, order, side=None):
    for i, s in enumerate(order):
        bit = (idx >> s) & 1
        if side is not None and i == 1:
            buf, side = lax.optimization_barrier((buf, side))
        recv = lax.ppermute(buf, axis, _partner(n, s))
        buf = jnp.where(
            bit == 0,
            jnp.concatenate([buf, recv], axis=-1),
            jnp.concatenate([recv, buf], axis=-1),
        )
    if side is not None:
        return buf, side
    return buf


def _pair_perm(n_row, n_col, bits):
    return [
        (r * n_col + c, r * n_col + (c ^ (1 << bits[r & 1])))
        for r in range(n_row)
        for c in range(n_col)
    ]


def _pair_bit(c, odd, bits):
    return (c >> jnp.where(odd == 0, bits[0], bits[1])) & 1


def _butterfly(x, axis, n):
    for s in range(_steps(n)):
        x = x + lax.ppermute(x, axis, _partner(n, s))
    return x


def shards(solution, residual, direction, gradient, left_factors, right_factors, ranks):
    left = left_factors[:, 0, 0]
    right = right_factors[:, 0, 0]
    rounds, tile, rank_max = left.shape
    rhs = direction.shape[1]
    t_local = residual.shape[3]
    n_col = tile // t_local
    n_row = tile // direction.shape[2]
    c = lax.axis_index("col")
    r = lax.axis_index("row")
    mask = (
        jnp.arange(rank_max, dtype=jnp.int32)[None, None, :] < ranks[:, 0, 0][:, None, None]
    ).astype(jnp.float32)
    g_local = jnp.sum(gradient * gradient, axis=(0, 2))
    coeffs = (
        jnp.einsum(
            "hn,anm->ahm",
            lax.all_gather(direction, "row", axis=2, tiled=True)[0],
            right,
            precision=HIGH,
        )
        * mask
    )

    def image_part(start, size):
        rows = lax.dynamic_slice_in_dim(left, start, size, axis=1)
        part = jnp.einsum("ahm,atm->aht", coeffs, rows, precision=HIGH)
        return part.reshape(rounds * rhs, size)

    k_col = _steps(n_col)
    grid = ("row", "col")
    odd = r & 1
    if k_col >= 3:
        ar_order = ([0, 1] + list(range(2, k_col)), [1, 0] + list(range(2, k_col)))
        res_order = ([2, 0, 1] + list(range(3, k_col)), [2, 1, 0] + list(range(3, k_col)))
    else:
        ar_order = (list(range(k_col)), list(range(k_col)))
        res_order = ar_order

    def steps(order, i):
        return (order[0][i], order[1][i])

    def doubling(buf, i_steps, order):
        for i in i_steps:
            bits = steps(order, i)
            recv = lax.ppermute(buf, grid, _pair_perm(n_row, n_col, bits))
            buf = _join_lanes(_pair_bit(c, odd, bits), buf, recv)
        return buf

    extra = jnp.zeros((8, t_local), jnp.float32).at[0, :rhs].set(g_local)
    res = jnp.concatenate([residual[:, 0].reshape(rounds * rhs, t_local), extra], axis=0)
    res = doubling(res, range(k_col - 1), res_order)
    bits0 = steps(ar_order, 0)
    bit = _pair_bit(c, odd, bits0)
    half = tile // 2
    send = image_part((1 - bit) * half, half)
    res, send = lax.optimization_barrier((res, send))
    keep = image_part(bit * half, half)
    got = lax.ppermute(send, grid, _pair_perm(n_row, n_col, bits0))
    res = doubling(res, range(k_col - 1, k_col), res_order)
    res, got = lax.optimization_barrier((res, got))
    gamma_col = jnp.sum(res[rounds * rhs].reshape(n_col, t_local)[:, :rhs], axis=0)
    blocks_res = res[: rounds * rhs].reshape(rounds, rhs, n_col, t_local)
    where = [
        [sum(((d >> s) & 1) << i for i, s in enumerate(order)) for d in range(n_col)]
        for order in res_order
    ]
    where = jnp.where(odd == 0, jnp.array(where[0]), jnp.array(where[1]))
    residual_full = jnp.take(blocks_res, where, axis=2).reshape(rounds, rhs, tile)
    back_res = jnp.einsum("aht,atm->ahm", residual_full, left, precision=HIGH) * mask
    buf = keep + got
    for i in range(1, k_col):
        bits = steps(ar_order, i)
        bit = _pair_bit(c, odd, bits)
        half = buf.shape[-1] // 2
        keep = lax.dynamic_slice_in_dim(buf, bit * half, half, axis=1)
        send = lax.dynamic_slice_in_dim(buf, (1 - bit) * half, half, axis=1)
        buf = keep + lax.ppermute(send, grid, _pair_perm(n_row, n_col, bits))
    buf, back_res = lax.optimization_barrier((buf, back_res))
    p_res = jnp.einsum("ahm,anm->hn", back_res, right, precision=HIGH)
    for j, i in enumerate(reversed(range(k_col))):
        bits = steps(ar_order, i)
        if j == min(2, k_col - 1):
            buf, p_res = lax.optimization_barrier((buf, p_res))
        recv = lax.ppermute(buf, grid, _pair_perm(n_row, n_col, bits))
        buf = _join_lanes(_pair_bit(c, odd, bits), buf, recv)
    summed = buf
    image_full = summed.reshape(rounds, rhs, tile)
    d_local = jnp.sum(image_full * image_full, axis=(0, 2))
    sums = _butterfly(jnp.stack([gamma_col, d_local]), "row", n_row)
    gamma = sums[0]
    delta = sums[1]
    alpha = gamma / delta
    solution_new = solution + alpha[None, :, None] * direction
    image_mine = lax.dynamic_slice_in_dim(image_full, c * t_local, t_local, axis=2)
    residual_new = residual - alpha[None, None, :, None] * image_mine[:, None]
    back_img = jnp.einsum("aht,atm->ahm", image_full, left, precision=HIGH) * mask
    p_img = jnp.einsum("ahm,anm->hn", back_img, right, precision=HIGH)
    partial_gradient = p_res - alpha[:, None] * p_img
    k_row = _steps(n_row)
    order = [_bitrev(p, k_row) for p in range(n_row)]
    blocks = partial_gradient.reshape(rhs, n_row, tile // n_row)[:, jnp.array(order)]
    gradient_new = _halve(blocks.reshape(rhs, tile), "row", n_row, r)[None]
    g_new = _butterfly(_butterfly(jnp.sum(gradient_new * gradient_new, axis=(0, 2)), "row", n_row), "col", n_col)
    beta = g_new / gamma
    direction_new = gradient_new + beta[None, :, None] * direction
    return (solution_new, residual_new, direction_new, gradient_new)


def solution(mesh):
    return jax.shard_map(
        shards,
        mesh=mesh,
        in_specs=(
            P("col", None, "row"),
            P(None, "row", None, "col"),
            P("col", None, "row"),
            P("col", None, "row"),
            P(None, "row", "col", None, None),
            P(None, "row", "col", None, None),
            P(None, "row", "col"),
        ),
        out_specs=(
            P("col", None, "row"),
            P(None, "row", None, "col"),
            P("col", None, "row"),
            P("col", None, "row"),
        ),
        check_vma=False,
    )
```

```python
import jax
import jax.numpy as jnp
from jax import lax
from jax.sharding import PartitionSpec as P

HIGH = lax.Precision.HIGH


def _steps(n):
    k = n.bit_length() - 1
    assert (1 << k) == n
    return k


def _partner(n, s):
    return [(i, i ^ (1 << s)) for i in range(n)]


def _bitrev(i, k):
    return int(format(i, f"0{k}b")[::-1], 2) if k else 0


def _halve(buf, axis, n, idx):
    return _halve_from(buf, axis, n, idx, 0)


def _halve_from(buf, axis, n, idx, first, side=None):
    for s in range(first, _steps(n)):
        bit = (idx >> s) & 1
        half = buf.shape[-1] // 2
        keep = lax.dynamic_slice_in_dim(buf, bit * half, half, axis=buf.ndim - 1)
        send = lax.dynamic_slice_in_dim(buf, (1 - bit) * half, half, axis=buf.ndim - 1)
        if side is not None and s == first + 1:
            send, side = lax.optimization_barrier((send, side))
        buf = keep + lax.ppermute(send, axis, _partner(n, s))
    if side is not None:
        return buf, side
    return buf


def _join_lanes(bit, mine, theirs):
    return jnp.where(
        bit == 0,
        jnp.concatenate([mine, theirs], axis=-1),
        jnp.concatenate([theirs, mine], axis=-1),
    )


def _double(buf, axis, n, idx, order, side=None):
    for i, s in enumerate(order):
        bit = (idx >> s) & 1
        if side is not None and i == 1:
            buf, side = lax.optimization_barrier((buf, side))
        recv = lax.ppermute(buf, axis, _partner(n, s))
        buf = jnp.where(
            bit == 0,
            jnp.concatenate([buf, recv], axis=-1),
            jnp.concatenate([recv, buf], axis=-1),
        )
    if side is not None:
        return buf, side
    return buf


def _pair_perm(n_row, n_col, bits):
    return [
        (r * n_col + c, r * n_col + (c ^ (1 << bits[r & 1])))
        for r in range(n_row)
        for c in range(n_col)
    ]


def _pair_bit(c, odd, bits):
    return (c >> jnp.where(odd == 0, bits[0], bits[1])) & 1


def _butterfly(x, axis, n):
    for s in range(_steps(n)):
        x = x + lax.ppermute(x, axis, _partner(n, s))
    return x


def shards(solution, residual, direction, gradient, left_factors, right_factors, ranks):
    left = left_factors[:, 0, 0]
    right = right_factors[:, 0, 0]
    rounds, tile, rank_max = left.shape
    rhs = direction.shape[1]
    t_local = residual.shape[3]
    n_col = tile // t_local
    n_row = tile // direction.shape[2]
    c = lax.axis_index("col")
    r = lax.axis_index("row")
    mask = (
        jnp.arange(rank_max, dtype=jnp.int32)[None, None, :] < ranks[:, 0, 0][:, None, None]
    ).astype(jnp.float32)
    g_local = jnp.sum(gradient * gradient, axis=(0, 2))
    coeffs = (
        jnp.einsum(
            "hn,anm->ahm",
            lax.all_gather(direction, "row", axis=2, tiled=True)[0],
            right,
            precision=HIGH,
        )
        * mask
    )

    def image_part(start, size):
        rows = lax.dynamic_slice_in_dim(left, start, size, axis=1)
        part = jnp.einsum("ahm,atm->aht", coeffs, rows, precision=HIGH)
        return part.reshape(rounds * rhs, size)

    k_col = _steps(n_col)
    grid = ("row", "col")
    odd = r & 1
    if k_col >= 3:
        ar_order = ([0, 1] + list(range(2, k_col)), [1, 0] + list(range(2, k_col)))
        res_order = ([2, 0, 1] + list(range(3, k_col)), [2, 1, 0] + list(range(3, k_col)))
    else:
        ar_order = (list(range(k_col)), list(range(k_col)))
        res_order = ar_order

    def steps(order, i):
        return (order[0][i], order[1][i])

    def doubling(buf, i_steps, order):
        for i in i_steps:
            bits = steps(order, i)
            recv = lax.ppermute(buf, grid, _pair_perm(n_row, n_col, bits))
            buf = _join_lanes(_pair_bit(c, odd, bits), buf, recv)
        return buf

    extra = jnp.zeros((8, t_local), jnp.float32).at[0, :rhs].set(g_local)
    res = jnp.concatenate([residual[:, 0].reshape(rounds * rhs, t_local), extra], axis=0)
    res = doubling(res, range(k_col - 1), res_order)
    bits0 = steps(ar_order, 0)
    bit = _pair_bit(c, odd, bits0)
    half = tile // 2
    send = image_part((1 - bit) * half, half)
    res, send = lax.optimization_barrier((res, send))
    keep = image_part(bit * half, half)
    got = lax.ppermute(send, grid, _pair_perm(n_row, n_col, bits0))
    res = doubling(res, range(k_col - 1, k_col), res_order)
    res, got = lax.optimization_barrier((res, got))
    gamma_col = jnp.sum(res[rounds * rhs].reshape(n_col, t_local)[:, :rhs], axis=0)
    blocks_res = res[: rounds * rhs].reshape(rounds, rhs, n_col, t_local)
    where = [
        [sum(((d >> s) & 1) << i for i, s in enumerate(order)) for d in range(n_col)]
        for order in res_order
    ]
    where = jnp.where(odd == 0, jnp.array(where[0]), jnp.array(where[1]))
    residual_full = jnp.take(blocks_res, where, axis=2).reshape(rounds, rhs, tile)
    back_res = jnp.einsum("aht,atm->ahm", residual_full, left, precision=HIGH) * mask
    buf = keep + got
    for i in range(1, k_col):
        bits = steps(ar_order, i)
        bit = _pair_bit(c, odd, bits)
        half = buf.shape[-1] // 2
        keep = lax.dynamic_slice_in_dim(buf, bit * half, half, axis=1)
        send = lax.dynamic_slice_in_dim(buf, (1 - bit) * half, half, axis=1)
        buf = keep + lax.ppermute(send, grid, _pair_perm(n_row, n_col, bits))
    buf, back_res = lax.optimization_barrier((buf, back_res))
    p_res = jnp.einsum("ahm,anm->hn", back_res, right, precision=HIGH)
    for j, i in enumerate(reversed(range(k_col))):
        bits = steps(ar_order, i)
        if j == min(2, k_col - 1):
            buf, p_res = lax.optimization_barrier((buf, p_res))
        recv = lax.ppermute(buf, grid, _pair_perm(n_row, n_col, bits))
        buf = _join_lanes(_pair_bit(c, odd, bits), buf, recv)
    summed = buf
    image_full = summed.reshape(rounds, rhs, tile)
    d_local = jnp.sum(image_full * image_full, axis=(0, 2))
    sums = _butterfly(jnp.stack([gamma_col, d_local]), "row", n_row)
    gamma = sums[0]
    delta = sums[1]
    alpha = gamma / delta
    solution_new = solution + alpha[None, :, None] * direction
    image_mine = lax.dynamic_slice_in_dim(image_full, c * t_local, t_local, axis=2)
    residual_new = residual - alpha[None, None, :, None] * image_mine[:, None]
    back_img = jnp.einsum("aht,atm->ahm", image_full, left, precision=HIGH) * mask
    p_img = jnp.einsum("ahm,anm->hn", back_img, right, precision=HIGH)
    partial_gradient = p_res - alpha[:, None] * p_img
    k_row = _steps(n_row)
    order = [_bitrev(p, k_row) for p in range(n_row)]
    blocks = partial_gradient.reshape(rhs, n_row, tile // n_row)[:, jnp.array(order)]
    buf = blocks.reshape(rhs, tile)
    for s in range(k_row):
        bit = (r >> s) & 1
        half = buf.shape[-1] // 2
        if s < k_row - 1:
            keep = lax.dynamic_slice_in_dim(buf, bit * half, half, axis=1)
            send = lax.dynamic_slice_in_dim(buf, (1 - bit) * half, half, axis=1)
        else:
            keep, send = buf, buf
        buf = keep + lax.ppermute(send, "row", _partner(n_row, s))
    g_row = jnp.sum(buf * buf, axis=1)
    for s in range(k_row - 1):
        g_row = g_row + lax.ppermute(g_row, "row", _partner(n_row, s))
    last = (r >> (k_row - 1)) & 1
    chunk = tile // n_row
    gradient_new = lax.dynamic_slice_in_dim(buf, last * chunk, chunk, axis=1)[None]
    g_new = _butterfly(g_row, "col", n_col)
    beta = g_new / gamma
    direction_new = gradient_new + beta[None, :, None] * direction
    return (solution_new, residual_new, direction_new, gradient_new)


def solution(mesh):
    return jax.shard_map(
        shards,
        mesh=mesh,
        in_specs=(
            P("col", None, "row"),
            P(None, "row", None, "col"),
            P("col", None, "row"),
            P("col", None, "row"),
            P(None, "row", "col", None, None),
            P(None, "row", "col", None, None),
            P(None, "row", "col"),
        ),
        out_specs=(
            P("col", None, "row"),
            P(None, "row", None, "col"),
            P("col", None, "row"),
            P("col", None, "row"),
        ),
        check_vma=False,
    )
```

```python
import jax
import jax.numpy as jnp
from jax import lax
from jax.sharding import PartitionSpec as P

HIGH = lax.Precision.HIGH


def _steps(n):
    k = n.bit_length() - 1
    assert (1 << k) == n
    return k


def _partner(n, s):
    return [(i, i ^ (1 << s)) for i in range(n)]


def _bitrev(i, k):
    return int(format(i, f"0{k}b")[::-1], 2) if k else 0


def _halve(buf, axis, n, idx):
    return _halve_from(buf, axis, n, idx, 0)


def _halve_from(buf, axis, n, idx, first, side=None):
    for s in range(first, _steps(n)):
        bit = (idx >> s) & 1
        half = buf.shape[-1] // 2
        keep = lax.dynamic_slice_in_dim(buf, bit * half, half, axis=buf.ndim - 1)
        send = lax.dynamic_slice_in_dim(buf, (1 - bit) * half, half, axis=buf.ndim - 1)
        if side is not None and s == first + 1:
            send, side = lax.optimization_barrier((send, side))
        buf = keep + lax.ppermute(send, axis, _partner(n, s))
    if side is not None:
        return buf, side
    return buf


def _join_lanes(bit, mine, theirs):
    return jnp.where(
        bit == 0,
        jnp.concatenate([mine, theirs], axis=-1),
        jnp.concatenate([theirs, mine], axis=-1),
    )


def _double(buf, axis, n, idx, order, side=None):
    for i, s in enumerate(order):
        bit = (idx >> s) & 1
        if side is not None and i == 1:
            buf, side = lax.optimization_barrier((buf, side))
        recv = lax.ppermute(buf, axis, _partner(n, s))
        buf = jnp.where(
            bit == 0,
            jnp.concatenate([buf, recv], axis=-1),
            jnp.concatenate([recv, buf], axis=-1),
        )
    if side is not None:
        return buf, side
    return buf


def _pair_perm(n_row, n_col, bits):
    return [
        (r * n_col + c, r * n_col + (c ^ (1 << bits[r & 1])))
        for r in range(n_row)
        for c in range(n_col)
    ]


def _pair_bit(c, odd, bits):
    return (c >> jnp.where(odd == 0, bits[0], bits[1])) & 1


def _radix4(x, axis, n):
    k = _steps(n)
    x = x + lax.ppermute(x, axis, _partner(n, 0))
    s = 1
    while s < k:
        if s + 1 < k:
            got = [lax.ppermute(x, axis, [(i, i ^ (m << s)) for i in range(n)]) for m in (1, 2, 3)]
            x = x + (got[0] + (got[1] + got[2]))
            s += 2
        else:
            x = x + lax.ppermute(x, axis, _partner(n, s))
            s += 1
    return x


def _butterfly(x, axis, n):
    for s in range(_steps(n)):
        x = x + lax.ppermute(x, axis, _partner(n, s))
    return x


def shards(solution, residual, direction, gradient, left_factors, right_factors, ranks):
    left = left_factors[:, 0, 0]
    right = right_factors[:, 0, 0]
    rounds, tile, rank_max = left.shape
    rhs = direction.shape[1]
    t_local = residual.shape[3]
    n_col = tile // t_local
    n_row = tile // direction.shape[2]
    c = lax.axis_index("col")
    r = lax.axis_index("row")
    mask = (
        jnp.arange(rank_max, dtype=jnp.int32)[None, None, :] < ranks[:, 0, 0][:, None, None]
    ).astype(jnp.float32)
    g_local = jnp.sum(gradient * gradient, axis=(0, 2))
    coeffs = (
        jnp.einsum(
            "hn,anm->ahm",
            lax.all_gather(direction, "row", axis=2, tiled=True)[0],
            right,
            precision=HIGH,
        )
        * mask
    )

    def image_part(start, size):
        rows = lax.dynamic_slice_in_dim(left, start, size, axis=1)
        part = jnp.einsum("ahm,atm->aht", coeffs, rows, precision=HIGH)
        return part.reshape(rounds * rhs, size)

    k_col = _steps(n_col)
    grid = ("row", "col")
    odd = r & 1
    if k_col >= 3:
        ar_order = ([0, 1] + list(range(2, k_col)), [1, 0] + list(range(2, k_col)))
        res_order = ([2, 0, 1] + list(range(3, k_col)), [2, 1, 0] + list(range(3, k_col)))
    else:
        ar_order = (list(range(k_col)), list(range(k_col)))
        res_order = ar_order

    def steps(order, i):
        return (order[0][i], order[1][i])

    def doubling(buf, i_steps, order):
        for i in i_steps:
            bits = steps(order, i)
            recv = lax.ppermute(buf, grid, _pair_perm(n_row, n_col, bits))
            buf = _join_lanes(_pair_bit(c, odd, bits), buf, recv)
        return buf

    extra = jnp.zeros((8, t_local), jnp.float32).at[0, :rhs].set(g_local)
    res = jnp.concatenate([residual[:, 0].reshape(rounds * rhs, t_local), extra], axis=0)
    res = doubling(res, range(k_col - 1), res_order)
    bits0 = steps(ar_order, 0)
    bit = _pair_bit(c, odd, bits0)
    half = tile // 2
    send = image_part((1 - bit) * half, half)
    res, send = lax.optimization_barrier((res, send))
    keep = image_part(bit * half, half)
    got = lax.ppermute(send, grid, _pair_perm(n_row, n_col, bits0))
    res = doubling(res, range(k_col - 1, k_col), res_order)
    res, got = lax.optimization_barrier((res, got))
    gamma_col = jnp.sum(res[rounds * rhs].reshape(n_col, t_local)[:, :rhs], axis=0)
    blocks_res = res[: rounds * rhs].reshape(rounds, rhs, n_col, t_local)
    where = [
        [sum(((d >> s) & 1) << i for i, s in enumerate(order)) for d in range(n_col)]
        for order in res_order
    ]
    where = jnp.where(odd == 0, jnp.array(where[0]), jnp.array(where[1]))
    residual_full = jnp.take(blocks_res, where, axis=2).reshape(rounds, rhs, tile)
    back_res = jnp.einsum("aht,atm->ahm", residual_full, left, precision=HIGH) * mask
    buf = keep + got
    for i in range(1, k_col):
        bits = steps(ar_order, i)
        bit = _pair_bit(c, odd, bits)
        half = buf.shape[-1] // 2
        keep = lax.dynamic_slice_in_dim(buf, bit * half, half, axis=1)
        send = lax.dynamic_slice_in_dim(buf, (1 - bit) * half, half, axis=1)
        buf = keep + lax.ppermute(send, grid, _pair_perm(n_row, n_col, bits))
    buf, back_res = lax.optimization_barrier((buf, back_res))
    p_res = jnp.einsum("ahm,anm->hn", back_res, right, precision=HIGH)
    for j, i in enumerate(reversed(range(k_col))):
        bits = steps(ar_order, i)
        if j == min(2, k_col - 1):
            buf, p_res = lax.optimization_barrier((buf, p_res))
        recv = lax.ppermute(buf, grid, _pair_perm(n_row, n_col, bits))
        buf = _join_lanes(_pair_bit(c, odd, bits), buf, recv)
    summed = buf
    image_full = summed.reshape(rounds, rhs, tile)
    d_local = jnp.sum(image_full * image_full, axis=(0, 2))
    sums = _butterfly(jnp.stack([gamma_col, d_local]), "row", n_row)
    gamma = sums[0]
    delta = sums[1]
    alpha = gamma / delta
    solution_new = solution + alpha[None, :, None] * direction
    image_mine = lax.dynamic_slice_in_dim(image_full, c * t_local, t_local, axis=2)
    residual_new = residual - alpha[None, None, :, None] * image_mine[:, None]
    back_img = jnp.einsum("aht,atm->ahm", image_full, left, precision=HIGH) * mask
    p_img = jnp.einsum("ahm,anm->hn", back_img, right, precision=HIGH)
    partial_gradient = p_res - alpha[:, None] * p_img
    k_row = _steps(n_row)
    order = [_bitrev(p, k_row) for p in range(n_row)]
    blocks = partial_gradient.reshape(rhs, n_row, tile // n_row)[:, jnp.array(order)]
    buf = blocks.reshape(rhs, tile)
    for s in range(k_row):
        bit = (r >> s) & 1
        half = buf.shape[-1] // 2
        if s < k_row - 1:
            keep = lax.dynamic_slice_in_dim(buf, bit * half, half, axis=1)
            send = lax.dynamic_slice_in_dim(buf, (1 - bit) * half, half, axis=1)
        else:
            keep, send = buf, buf
        buf = keep + lax.ppermute(send, "row", _partner(n_row, s))
    g_row = jnp.sum(buf * buf, axis=1)
    for s in range(k_row - 1):
        g_row = g_row + lax.ppermute(g_row, "row", _partner(n_row, s))
    last = (r >> (k_row - 1)) & 1
    chunk = tile // n_row
    gradient_new = lax.dynamic_slice_in_dim(buf, last * chunk, chunk, axis=1)[None]
    g_new = _radix4(g_row, "col", n_col)
    beta = g_new / gamma
    direction_new = gradient_new + beta[None, :, None] * direction
    return (solution_new, residual_new, direction_new, gradient_new)


def solution(mesh):
    return jax.shard_map(
        shards,
        mesh=mesh,
        in_specs=(
            P("col", None, "row"),
            P(None, "row", None, "col"),
            P("col", None, "row"),
            P("col", None, "row"),
            P(None, "row", "col", None, None),
            P(None, "row", "col", None, None),
            P(None, "row", "col"),
        ),
        out_specs=(
            P("col", None, "row"),
            P(None, "row", None, "col"),
            P("col", None, "row"),
            P("col", None, "row"),
        ),
        check_vma=False,
    )
```

```python
import jax
import jax.numpy as jnp
from jax import lax
from jax.sharding import PartitionSpec as P

HIGH = lax.Precision.HIGH


def _steps(n):
    k = n.bit_length() - 1
    assert (1 << k) == n
    return k


def _partner(n, s):
    return [(i, i ^ (1 << s)) for i in range(n)]


def _bitrev(i, k):
    return int(format(i, f"0{k}b")[::-1], 2) if k else 0


def _halve(buf, axis, n, idx):
    return _halve_from(buf, axis, n, idx, 0)


def _halve_from(buf, axis, n, idx, first, side=None):
    for s in range(first, _steps(n)):
        bit = (idx >> s) & 1
        half = buf.shape[-1] // 2
        keep = lax.dynamic_slice_in_dim(buf, bit * half, half, axis=buf.ndim - 1)
        send = lax.dynamic_slice_in_dim(buf, (1 - bit) * half, half, axis=buf.ndim - 1)
        if side is not None and s == first + 1:
            send, side = lax.optimization_barrier((send, side))
        buf = keep + lax.ppermute(send, axis, _partner(n, s))
    if side is not None:
        return buf, side
    return buf


def _join_lanes(bit, mine, theirs):
    return jnp.where(
        bit == 0,
        jnp.concatenate([mine, theirs], axis=-1),
        jnp.concatenate([theirs, mine], axis=-1),
    )


def _double(buf, axis, n, idx, order, side=None):
    for i, s in enumerate(order):
        bit = (idx >> s) & 1
        if side is not None and i == 1:
            buf, side = lax.optimization_barrier((buf, side))
        recv = lax.ppermute(buf, axis, _partner(n, s))
        buf = jnp.where(
            bit == 0,
            jnp.concatenate([buf, recv], axis=-1),
            jnp.concatenate([recv, buf], axis=-1),
        )
    if side is not None:
        return buf, side
    return buf


def _pair_perm(n_row, n_col, bits):
    return [
        (r * n_col + c, r * n_col + (c ^ (1 << bits[r & 1])))
        for r in range(n_row)
        for c in range(n_col)
    ]


def _pair_bit(c, odd, bits):
    return (c >> jnp.where(odd == 0, bits[0], bits[1])) & 1


def _radix4(x, axis, n):
    k = _steps(n)
    x = x + lax.ppermute(x, axis, _partner(n, 0))
    s = 1
    while s < k:
        if s + 1 < k:
            got = [lax.ppermute(x, axis, [(i, i ^ (m << s)) for i in range(n)]) for m in (1, 2, 3)]
            x = x + (got[0] + (got[1] + got[2]))
            s += 2
        else:
            x = x + lax.ppermute(x, axis, _partner(n, s))
            s += 1
    return x


def _one_round(x, axis, n):
    k = _steps(n)
    s = 0
    while s < k:
        w = min(3, k - s)
        got = [lax.ppermute(x, axis, [(i, i ^ (m << s)) for i in range(n)]) for m in range(1, 1 << w)]
        total = got[0]
        for g in got[1:]:
            total = total + g
        x = x + total
        s += w
    return x


def _butterfly(x, axis, n):
    for s in range(_steps(n)):
        x = x + lax.ppermute(x, axis, _partner(n, s))
    return x


def shards(solution, residual, direction, gradient, left_factors, right_factors, ranks):
    left = left_factors[:, 0, 0]
    right = right_factors[:, 0, 0]
    rounds, tile, rank_max = left.shape
    rhs = direction.shape[1]
    t_local = residual.shape[3]
    n_col = tile // t_local
    n_row = tile // direction.shape[2]
    c = lax.axis_index("col")
    r = lax.axis_index("row")
    mask = (
        jnp.arange(rank_max, dtype=jnp.int32)[None, None, :] < ranks[:, 0, 0][:, None, None]
    ).astype(jnp.float32)
    g_local = jnp.sum(gradient * gradient, axis=(0, 2))
    coeffs = (
        jnp.einsum(
            "hn,anm->ahm",
            lax.all_gather(direction, "row", axis=2, tiled=True)[0],
            right,
            precision=HIGH,
        )
        * mask
    )

    def image_part(start, size):
        rows = lax.dynamic_slice_in_dim(left, start, size, axis=1)
        part = jnp.einsum("ahm,atm->aht", coeffs, rows, precision=HIGH)
        return part.reshape(rounds * rhs, size)

    k_col = _steps(n_col)
    grid = ("row", "col")
    odd = r & 1
    if k_col >= 3:
        ar_order = ([0, 1] + list(range(2, k_col)), [1, 0] + list(range(2, k_col)))
        res_order = ([2, 0, 1] + list(range(3, k_col)), [2, 1, 0] + list(range(3, k_col)))
    else:
        ar_order = (list(range(k_col)), list(range(k_col)))
        res_order = ar_order

    def steps(order, i):
        return (order[0][i], order[1][i])

    def doubling(buf, i_steps, order):
        for i in i_steps:
            bits = steps(order, i)
            recv = lax.ppermute(buf, grid, _pair_perm(n_row, n_col, bits))
            buf = _join_lanes(_pair_bit(c, odd, bits), buf, recv)
        return buf

    extra = jnp.zeros((8, t_local), jnp.float32).at[0, :rhs].set(g_local)
    res = jnp.concatenate([residual[:, 0].reshape(rounds * rhs, t_local), extra], axis=0)
    res = doubling(res, range(k_col - 1), res_order)
    bits0 = steps(ar_order, 0)
    bit = _pair_bit(c, odd, bits0)
    half = tile // 2
    send = image_part((1 - bit) * half, half)
    res, send = lax.optimization_barrier((res, send))
    keep = image_part(bit * half, half)
    got = lax.ppermute(send, grid, _pair_perm(n_row, n_col, bits0))
    res = doubling(res, range(k_col - 1, k_col), res_order)
    res, got = lax.optimization_barrier((res, got))
    gamma_col = jnp.sum(res[rounds * rhs].reshape(n_col, t_local)[:, :rhs], axis=0)
    blocks_res = res[: rounds * rhs].reshape(rounds, rhs, n_col, t_local)
    where = [
        [sum(((d >> s) & 1) << i for i, s in enumerate(order)) for d in range(n_col)]
        for order in res_order
    ]
    where = jnp.where(odd == 0, jnp.array(where[0]), jnp.array(where[1]))
    residual_full = jnp.take(blocks_res, where, axis=2).reshape(rounds, rhs, tile)
    back_res = jnp.einsum("aht,atm->ahm", residual_full, left, precision=HIGH) * mask
    buf = keep + got
    for i in range(1, k_col):
        bits = steps(ar_order, i)
        bit = _pair_bit(c, odd, bits)
        half = buf.shape[-1] // 2
        keep = lax.dynamic_slice_in_dim(buf, bit * half, half, axis=1)
        send = lax.dynamic_slice_in_dim(buf, (1 - bit) * half, half, axis=1)
        buf = keep + lax.ppermute(send, grid, _pair_perm(n_row, n_col, bits))
    buf, back_res = lax.optimization_barrier((buf, back_res))
    p_res = jnp.einsum("ahm,anm->hn", back_res, right, precision=HIGH)
    for j, i in enumerate(reversed(range(k_col))):
        bits = steps(ar_order, i)
        if j == min(2, k_col - 1):
            buf, p_res = lax.optimization_barrier((buf, p_res))
        recv = lax.ppermute(buf, grid, _pair_perm(n_row, n_col, bits))
        buf = _join_lanes(_pair_bit(c, odd, bits), buf, recv)
    summed = buf
    image_full = summed.reshape(rounds, rhs, tile)
    d_local = jnp.sum(image_full * image_full, axis=(0, 2))
    sums = _butterfly(jnp.stack([gamma_col, d_local]), "row", n_row)
    gamma = sums[0]
    delta = sums[1]
    alpha = gamma / delta
    solution_new = solution + alpha[None, :, None] * direction
    image_mine = lax.dynamic_slice_in_dim(image_full, c * t_local, t_local, axis=2)
    residual_new = residual - alpha[None, None, :, None] * image_mine[:, None]
    back_img = jnp.einsum("aht,atm->ahm", image_full, left, precision=HIGH) * mask
    p_img = jnp.einsum("ahm,anm->hn", back_img, right, precision=HIGH)
    partial_gradient = p_res - alpha[:, None] * p_img
    k_row = _steps(n_row)
    order = [_bitrev(p, k_row) for p in range(n_row)]
    blocks = partial_gradient.reshape(rhs, n_row, tile // n_row)[:, jnp.array(order)]
    buf = blocks.reshape(rhs, tile)
    for s in range(k_row):
        bit = (r >> s) & 1
        half = buf.shape[-1] // 2
        if s < k_row - 1:
            keep = lax.dynamic_slice_in_dim(buf, bit * half, half, axis=1)
            send = lax.dynamic_slice_in_dim(buf, (1 - bit) * half, half, axis=1)
        else:
            keep, send = buf, buf
        buf = keep + lax.ppermute(send, "row", _partner(n_row, s))
    g_row = jnp.sum(buf * buf, axis=1)
    for s in range(k_row - 1):
        g_row = g_row + lax.ppermute(g_row, "row", _partner(n_row, s))
    last = (r >> (k_row - 1)) & 1
    chunk = tile // n_row
    gradient_new = lax.dynamic_slice_in_dim(buf, last * chunk, chunk, axis=1)[None]
    g_new = _one_round(g_row, "col", n_col)
    beta = g_new / gamma
    direction_new = gradient_new + beta[None, :, None] * direction
    return (solution_new, residual_new, direction_new, gradient_new)


def solution(mesh):
    return jax.shard_map(
        shards,
        mesh=mesh,
        in_specs=(
            P("col", None, "row"),
            P(None, "row", None, "col"),
            P("col", None, "row"),
            P("col", None, "row"),
            P(None, "row", "col", None, None),
            P(None, "row", "col", None, None),
            P(None, "row", "col"),
        ),
        out_specs=(
            P("col", None, "row"),
            P(None, "row", None, "col"),
            P("col", None, "row"),
            P("col", None, "row"),
        ),
        check_vma=False,
    )
```

```python
import jax
import jax.numpy as jnp
from jax import lax
from jax.sharding import PartitionSpec as P

HIGH = lax.Precision.HIGH


def _steps(n):
    k = n.bit_length() - 1
    assert (1 << k) == n
    return k


def _partner(n, s):
    return [(i, i ^ (1 << s)) for i in range(n)]


def _bitrev(i, k):
    return int(format(i, f"0{k}b")[::-1], 2) if k else 0


def _halve(buf, axis, n, idx):
    return _halve_from(buf, axis, n, idx, 0)


def _halve_from(buf, axis, n, idx, first, side=None):
    for s in range(first, _steps(n)):
        bit = (idx >> s) & 1
        half = buf.shape[-1] // 2
        keep = lax.dynamic_slice_in_dim(buf, bit * half, half, axis=buf.ndim - 1)
        send = lax.dynamic_slice_in_dim(buf, (1 - bit) * half, half, axis=buf.ndim - 1)
        if side is not None and s == first + 1:
            send, side = lax.optimization_barrier((send, side))
        buf = keep + lax.ppermute(send, axis, _partner(n, s))
    if side is not None:
        return buf, side
    return buf


def _join_lanes(bit, mine, theirs):
    return jnp.where(
        bit == 0,
        jnp.concatenate([mine, theirs], axis=-1),
        jnp.concatenate([theirs, mine], axis=-1),
    )


def _double(buf, axis, n, idx, order, side=None):
    for i, s in enumerate(order):
        bit = (idx >> s) & 1
        if side is not None and i == 1:
            buf, side = lax.optimization_barrier((buf, side))
        recv = lax.ppermute(buf, axis, _partner(n, s))
        buf = jnp.where(
            bit == 0,
            jnp.concatenate([buf, recv], axis=-1),
            jnp.concatenate([recv, buf], axis=-1),
        )
    if side is not None:
        return buf, side
    return buf


def _pair_perm(n_row, n_col, bits):
    return [
        (r * n_col + c, r * n_col + (c ^ (1 << bits[r & 1])))
        for r in range(n_row)
        for c in range(n_col)
    ]


def _pair_bit(c, odd, bits):
    return (c >> jnp.where(odd == 0, bits[0], bits[1])) & 1


def _radix4(x, axis, n):
    k = _steps(n)
    x = x + lax.ppermute(x, axis, _partner(n, 0))
    s = 1
    while s < k:
        if s + 1 < k:
            got = [lax.ppermute(x, axis, [(i, i ^ (m << s)) for i in range(n)]) for m in (1, 2, 3)]
            x = x + (got[0] + (got[1] + got[2]))
            s += 2
        else:
            x = x + lax.ppermute(x, axis, _partner(n, s))
            s += 1
    return x


def _radix4_low(x, axis, n):
    k = _steps(n)
    s = 0
    while s < k:
        if s + 1 < k:
            got = [lax.ppermute(x, axis, [(i, i ^ (m << s)) for i in range(n)]) for m in (1, 2, 3)]
            x = x + (got[0] + (got[1] + got[2]))
            s += 2
        else:
            x = x + lax.ppermute(x, axis, _partner(n, s))
            s += 1
    return x


def _butterfly(x, axis, n):
    for s in range(_steps(n)):
        x = x + lax.ppermute(x, axis, _partner(n, s))
    return x


def shards(solution, residual, direction, gradient, left_factors, right_factors, ranks):
    left = left_factors[:, 0, 0]
    right = right_factors[:, 0, 0]
    rounds, tile, rank_max = left.shape
    rhs = direction.shape[1]
    t_local = residual.shape[3]
    n_col = tile // t_local
    n_row = tile // direction.shape[2]
    c = lax.axis_index("col")
    r = lax.axis_index("row")
    mask = (
        jnp.arange(rank_max, dtype=jnp.int32)[None, None, :] < ranks[:, 0, 0][:, None, None]
    ).astype(jnp.float32)
    g_local = jnp.sum(gradient * gradient, axis=(0, 2))
    coeffs = (
        jnp.einsum(
            "hn,anm->ahm",
            lax.all_gather(direction, "row", axis=2, tiled=True)[0],
            right,
            precision=HIGH,
        )
        * mask
    )

    def image_part(start, size):
        rows = lax.dynamic_slice_in_dim(left, start, size, axis=1)
        part = jnp.einsum("ahm,atm->aht", coeffs, rows, precision=HIGH)
        return part.reshape(rounds * rhs, size)

    k_col = _steps(n_col)
    grid = ("row", "col")
    odd = r & 1
    if k_col >= 3:
        ar_order = ([0, 1] + list(range(2, k_col)), [1, 0] + list(range(2, k_col)))
        res_order = ([2, 0, 1] + list(range(3, k_col)), [2, 1, 0] + list(range(3, k_col)))
    else:
        ar_order = (list(range(k_col)), list(range(k_col)))
        res_order = ar_order

    def steps(order, i):
        return (order[0][i], order[1][i])

    def doubling(buf, i_steps, order):
        for i in i_steps:
            bits = steps(order, i)
            recv = lax.ppermute(buf, grid, _pair_perm(n_row, n_col, bits))
            buf = _join_lanes(_pair_bit(c, odd, bits), buf, recv)
        return buf

    extra = jnp.zeros((8, t_local), jnp.float32).at[0, :rhs].set(g_local)
    res = jnp.concatenate([residual[:, 0].reshape(rounds * rhs, t_local), extra], axis=0)
    res = doubling(res, range(k_col - 1), res_order)
    bits0 = steps(ar_order, 0)
    bit = _pair_bit(c, odd, bits0)
    half = tile // 2
    send = image_part((1 - bit) * half, half)
    res, send = lax.optimization_barrier((res, send))
    keep = image_part(bit * half, half)
    got = lax.ppermute(send, grid, _pair_perm(n_row, n_col, bits0))
    res = doubling(res, range(k_col - 1, k_col), res_order)
    res, got = lax.optimization_barrier((res, got))
    gamma_col = jnp.sum(res[rounds * rhs].reshape(n_col, t_local)[:, :rhs], axis=0)
    blocks_res = res[: rounds * rhs].reshape(rounds, rhs, n_col, t_local)
    where = [
        [sum(((d >> s) & 1) << i for i, s in enumerate(order)) for d in range(n_col)]
        for order in res_order
    ]
    where = jnp.where(odd == 0, jnp.array(where[0]), jnp.array(where[1]))
    residual_full = jnp.take(blocks_res, where, axis=2).reshape(rounds, rhs, tile)
    back_res = jnp.einsum("aht,atm->ahm", residual_full, left, precision=HIGH) * mask
    buf = keep + got
    for i in range(1, k_col):
        bits = steps(ar_order, i)
        bit = _pair_bit(c, odd, bits)
        half = buf.shape[-1] // 2
        keep = lax.dynamic_slice_in_dim(buf, bit * half, half, axis=1)
        send = lax.dynamic_slice_in_dim(buf, (1 - bit) * half, half, axis=1)
        buf = keep + lax.ppermute(send, grid, _pair_perm(n_row, n_col, bits))
    buf, back_res = lax.optimization_barrier((buf, back_res))
    p_res = jnp.einsum("ahm,anm->hn", back_res, right, precision=HIGH)
    for j, i in enumerate(reversed(range(k_col))):
        bits = steps(ar_order, i)
        if j == min(2, k_col - 1):
            buf, p_res = lax.optimization_barrier((buf, p_res))
        recv = lax.ppermute(buf, grid, _pair_perm(n_row, n_col, bits))
        buf = _join_lanes(_pair_bit(c, odd, bits), buf, recv)
    summed = buf
    image_full = summed.reshape(rounds, rhs, tile)
    d_local = jnp.sum(image_full * image_full, axis=(0, 2))
    sums = _radix4_low(jnp.stack([gamma_col, d_local]), "row", n_row)
    gamma = sums[0]
    delta = sums[1]
    alpha = gamma / delta
    solution_new = solution + alpha[None, :, None] * direction
    image_mine = lax.dynamic_slice_in_dim(image_full, c * t_local, t_local, axis=2)
    residual_new = residual - alpha[None, None, :, None] * image_mine[:, None]
    back_img = jnp.einsum("aht,atm->ahm", image_full, left, precision=HIGH) * mask
    p_img = jnp.einsum("ahm,anm->hn", back_img, right, precision=HIGH)
    partial_gradient = p_res - alpha[:, None] * p_img
    k_row = _steps(n_row)
    order = [_bitrev(p, k_row) for p in range(n_row)]
    blocks = partial_gradient.reshape(rhs, n_row, tile // n_row)[:, jnp.array(order)]
    buf = blocks.reshape(rhs, tile)
    for s in range(k_row):
        bit = (r >> s) & 1
        half = buf.shape[-1] // 2
        if s < k_row - 1:
            keep = lax.dynamic_slice_in_dim(buf, bit * half, half, axis=1)
            send = lax.dynamic_slice_in_dim(buf, (1 - bit) * half, half, axis=1)
        else:
            keep, send = buf, buf
        buf = keep + lax.ppermute(send, "row", _partner(n_row, s))
    g_row = jnp.sum(buf * buf, axis=1)
    for s in range(k_row - 1):
        g_row = g_row + lax.ppermute(g_row, "row", _partner(n_row, s))
    last = (r >> (k_row - 1)) & 1
    chunk = tile // n_row
    gradient_new = lax.dynamic_slice_in_dim(buf, last * chunk, chunk, axis=1)[None]
    g_new = _radix4(g_row, "col", n_col)
    beta = g_new / gamma
    direction_new = gradient_new + beta[None, :, None] * direction
    return (solution_new, residual_new, direction_new, gradient_new)


def solution(mesh):
    return jax.shard_map(
        shards,
        mesh=mesh,
        in_specs=(
            P("col", None, "row"),
            P(None, "row", None, "col"),
            P("col", None, "row"),
            P("col", None, "row"),
            P(None, "row", "col", None, None),
            P(None, "row", "col", None, None),
            P(None, "row", "col"),
        ),
        out_specs=(
            P("col", None, "row"),
            P(None, "row", None, "col"),
            P("col", None, "row"),
            P("col", None, "row"),
        ),
        check_vma=False,
    )
```

```python
import jax
import jax.numpy as jnp
from jax import lax
from jax.sharding import PartitionSpec as P

HIGH = lax.Precision.HIGH


def _steps(n):
    k = n.bit_length() - 1
    assert (1 << k) == n
    return k


def _partner(n, s):
    return [(i, i ^ (1 << s)) for i in range(n)]


def _bitrev(i, k):
    return int(format(i, f"0{k}b")[::-1], 2) if k else 0


def _halve(buf, axis, n, idx):
    return _halve_from(buf, axis, n, idx, 0)


def _halve_from(buf, axis, n, idx, first, side=None):
    for s in range(first, _steps(n)):
        bit = (idx >> s) & 1
        half = buf.shape[-1] // 2
        keep = lax.dynamic_slice_in_dim(buf, bit * half, half, axis=buf.ndim - 1)
        send = lax.dynamic_slice_in_dim(buf, (1 - bit) * half, half, axis=buf.ndim - 1)
        if side is not None and s == first + 1:
            send, side = lax.optimization_barrier((send, side))
        buf = keep + lax.ppermute(send, axis, _partner(n, s))
    if side is not None:
        return buf, side
    return buf


def _join_lanes(bit, mine, theirs):
    return jnp.where(
        bit == 0,
        jnp.concatenate([mine, theirs], axis=-1),
        jnp.concatenate([theirs, mine], axis=-1),
    )


def _double(buf, axis, n, idx, order, side=None):
    for i, s in enumerate(order):
        bit = (idx >> s) & 1
        if side is not None and i == 1:
            buf, side = lax.optimization_barrier((buf, side))
        recv = lax.ppermute(buf, axis, _partner(n, s))
        buf = jnp.where(
            bit == 0,
            jnp.concatenate([buf, recv], axis=-1),
            jnp.concatenate([recv, buf], axis=-1),
        )
    if side is not None:
        return buf, side
    return buf


def _pair_perm(n_row, n_col, bits):
    return [
        (r * n_col + c, r * n_col + (c ^ (1 << bits[r & 1])))
        for r in range(n_row)
        for c in range(n_col)
    ]


def _pair_bit(c, odd, bits):
    return (c >> jnp.where(odd == 0, bits[0], bits[1])) & 1


def _radix4(x, axis, n):
    k = _steps(n)
    x = x + lax.ppermute(x, axis, _partner(n, 0))
    s = 1
    while s < k:
        if s + 1 < k:
            got = [lax.ppermute(x, axis, [(i, i ^ (m << s)) for i in range(n)]) for m in (1, 2, 3)]
            x = x + (got[0] + (got[1] + got[2]))
            s += 2
        else:
            x = x + lax.ppermute(x, axis, _partner(n, s))
            s += 1
    return x


def _radix4_low(x, axis, n):
    k = _steps(n)
    s = 0
    while s < k:
        if s + 1 < k:
            got = [lax.ppermute(x, axis, [(i, i ^ (m << s)) for i in range(n)]) for m in (1, 2, 3)]
            x = x + (got[0] + (got[1] + got[2]))
            s += 2
        else:
            x = x + lax.ppermute(x, axis, _partner(n, s))
            s += 1
    return x


def _butterfly(x, axis, n):
    for s in range(_steps(n)):
        x = x + lax.ppermute(x, axis, _partner(n, s))
    return x


def shards(solution, residual, direction, gradient, left_factors, right_factors, ranks):
    left = left_factors[:, 0, 0]
    right = right_factors[:, 0, 0]
    rounds, tile, rank_max = left.shape
    rhs = direction.shape[1]
    t_local = residual.shape[3]
    n_col = tile // t_local
    n_row = tile // direction.shape[2]
    c = lax.axis_index("col")
    r = lax.axis_index("row")
    mask = (
        jnp.arange(rank_max, dtype=jnp.int32)[None, None, :] < ranks[:, 0, 0][:, None, None]
    ).astype(jnp.float32)
    g_local = jnp.sum(gradient * gradient, axis=(0, 2))
    coeffs = (
        jnp.einsum(
            "hn,anm->ahm",
            lax.all_gather(direction, "row", axis=2, tiled=True)[0],
            right,
            precision=HIGH,
        )
        * mask
    )

    def image_part(start, size):
        rows = lax.dynamic_slice_in_dim(left, start, size, axis=1)
        part = jnp.einsum("ahm,atm->aht", coeffs, rows, precision=HIGH)
        return part.reshape(rounds * rhs, size)

    k_col = _steps(n_col)
    grid = ("row", "col")
    odd = r & 1
    if k_col >= 3:
        ar_order = ([0, 1] + list(range(2, k_col)), [1, 0] + list(range(2, k_col)))
        res_order = ([2, 0, 1] + list(range(3, k_col)), [2, 1, 0] + list(range(3, k_col)))
    else:
        ar_order = (list(range(k_col)), list(range(k_col)))
        res_order = ar_order

    def steps(order, i):
        return (order[0][i], order[1][i])

    def doubling(buf, i_steps, order):
        for i in i_steps:
            bits = steps(order, i)
            recv = lax.ppermute(buf, grid, _pair_perm(n_row, n_col, bits))
            buf = _join_lanes(_pair_bit(c, odd, bits), buf, recv)
        return buf

    extra = jnp.zeros((8, t_local), jnp.float32).at[0, :rhs].set(g_local)
    res = jnp.concatenate([residual[:, 0].reshape(rounds * rhs, t_local), extra], axis=0)
    res = doubling(res, range(k_col - 1), res_order)
    bits0 = steps(ar_order, 0)
    bit = _pair_bit(c, odd, bits0)
    half = tile // 2
    send = image_part((1 - bit) * half, half)
    res, send = lax.optimization_barrier((res, send))
    keep = image_part(bit * half, half)
    got = lax.ppermute(send, grid, _pair_perm(n_row, n_col, bits0))
    res = doubling(res, range(k_col - 1, k_col), res_order)
    res, got = lax.optimization_barrier((res, got))
    gamma_col = jnp.sum(res[rounds * rhs].reshape(n_col, t_local)[:, :rhs], axis=0)
    blocks_res = res[: rounds * rhs].reshape(rounds, rhs, n_col, t_local)
    where = [
        [sum(((d >> s) & 1) << i for i, s in enumerate(order)) for d in range(n_col)]
        for order in res_order
    ]
    where = jnp.where(odd == 0, jnp.array(where[0]), jnp.array(where[1]))
    residual_full = jnp.take(blocks_res, where, axis=2).reshape(rounds, rhs, tile)
    back_res = jnp.einsum("aht,atm->ahm", residual_full, left, precision=HIGH) * mask
    buf = keep + got
    for i in range(1, k_col):
        bits = steps(ar_order, i)
        bit = _pair_bit(c, odd, bits)
        half = buf.shape[-1] // 2
        keep = lax.dynamic_slice_in_dim(buf, bit * half, half, axis=1)
        send = lax.dynamic_slice_in_dim(buf, (1 - bit) * half, half, axis=1)
        buf = keep + lax.ppermute(send, grid, _pair_perm(n_row, n_col, bits))
    buf, back_res = lax.optimization_barrier((buf, back_res))
    p_res = jnp.einsum("ahm,anm->hn", back_res, right, precision=HIGH)
    for j, i in enumerate(reversed(range(k_col))):
        bits = steps(ar_order, i)
        if j == min(2, k_col - 1):
            buf, p_res = lax.optimization_barrier((buf, p_res))
        recv = lax.ppermute(buf, grid, _pair_perm(n_row, n_col, bits))
        buf = _join_lanes(_pair_bit(c, odd, bits), buf, recv)
    summed = buf
    image_full = summed.reshape(rounds, rhs, tile)
    d_local = jnp.sum(image_full * image_full, axis=(0, 2))
    sums = _butterfly(jnp.stack([gamma_col, d_local]), "row", n_row)
    gamma = sums[0]
    delta = sums[1]
    alpha = gamma / delta
    solution_new = solution + alpha[None, :, None] * direction
    image_mine = lax.dynamic_slice_in_dim(image_full, c * t_local, t_local, axis=2)
    residual_new = residual - alpha[None, None, :, None] * image_mine[:, None]
    back_img = jnp.einsum("aht,atm->ahm", image_full, left, precision=HIGH) * mask
    p_img = jnp.einsum("ahm,anm->hn", back_img, right, precision=HIGH)
    partial_gradient = p_res - alpha[:, None] * p_img
    k_row = _steps(n_row)
    order = [_bitrev(p, k_row) for p in range(n_row)]
    blocks = partial_gradient.reshape(rhs, n_row, tile // n_row)[:, jnp.array(order)]
    buf = blocks.reshape(rhs, tile)
    for s in range(k_row):
        bit = (r >> s) & 1
        half = buf.shape[-1] // 2
        if s < k_row - 1:
            keep = lax.dynamic_slice_in_dim(buf, bit * half, half, axis=1)
            send = lax.dynamic_slice_in_dim(buf, (1 - bit) * half, half, axis=1)
        else:
            keep, send = buf, buf
        buf = keep + lax.ppermute(send, "row", _partner(n_row, s))
    g_row = jnp.sum(buf * buf, axis=1)
    for s in range(k_row - 1):
        g_row = g_row + lax.ppermute(g_row, "row", _partner(n_row, s))
    last = (r >> (k_row - 1)) & 1
    chunk = tile // n_row
    gradient_new = lax.dynamic_slice_in_dim(buf, last * chunk, chunk, axis=1)[None]
    g_new = _radix4_low(g_row, "col", n_col)
    beta = g_new / gamma
    direction_new = gradient_new + beta[None, :, None] * direction
    return (solution_new, residual_new, direction_new, gradient_new)


def solution(mesh):
    return jax.shard_map(
        shards,
        mesh=mesh,
        in_specs=(
            P("col", None, "row"),
            P(None, "row", None, "col"),
            P("col", None, "row"),
            P("col", None, "row"),
            P(None, "row", "col", None, None),
            P(None, "row", "col", None, None),
            P(None, "row", "col"),
        ),
        out_specs=(
            P("col", None, "row"),
            P(None, "row", None, "col"),
            P("col", None, "row"),
            P("col", None, "row"),
        ),
        check_vma=False,
    )
```

```python
import jax
import jax.numpy as jnp
from jax import lax
from jax.sharding import PartitionSpec as P

HIGH = lax.Precision.HIGH


def _steps(n):
    k = n.bit_length() - 1
    assert (1 << k) == n
    return k


def _partner(n, s):
    return [(i, i ^ (1 << s)) for i in range(n)]


def _bitrev(i, k):
    return int(format(i, f"0{k}b")[::-1], 2) if k else 0


def _halve(buf, axis, n, idx):
    return _halve_from(buf, axis, n, idx, 0)


def _halve_from(buf, axis, n, idx, first, side=None):
    for s in range(first, _steps(n)):
        bit = (idx >> s) & 1
        half = buf.shape[-1] // 2
        keep = lax.dynamic_slice_in_dim(buf, bit * half, half, axis=buf.ndim - 1)
        send = lax.dynamic_slice_in_dim(buf, (1 - bit) * half, half, axis=buf.ndim - 1)
        if side is not None and s == first + 1:
            send, side = lax.optimization_barrier((send, side))
        buf = keep + lax.ppermute(send, axis, _partner(n, s))
    if side is not None:
        return buf, side
    return buf


def _join_lanes(bit, mine, theirs):
    return jnp.where(
        bit == 0,
        jnp.concatenate([mine, theirs], axis=-1),
        jnp.concatenate([theirs, mine], axis=-1),
    )


def _double(buf, axis, n, idx, order, side=None):
    for i, s in enumerate(order):
        bit = (idx >> s) & 1
        if side is not None and i == 1:
            buf, side = lax.optimization_barrier((buf, side))
        recv = lax.ppermute(buf, axis, _partner(n, s))
        buf = jnp.where(
            bit == 0,
            jnp.concatenate([buf, recv], axis=-1),
            jnp.concatenate([recv, buf], axis=-1),
        )
    if side is not None:
        return buf, side
    return buf


def _pair_perm(n_row, n_col, bits):
    return [
        (r * n_col + c, r * n_col + (c ^ (1 << bits[r & 1])))
        for r in range(n_row)
        for c in range(n_col)
    ]


def _pair_bit(c, odd, bits):
    return (c >> jnp.where(odd == 0, bits[0], bits[1])) & 1


def _radix4(x, axis, n):
    k = _steps(n)
    s = 1
    while s < k:
        if s + 1 < k:
            got = [lax.ppermute(x, axis, [(i, i ^ (m << s)) for i in range(n)]) for m in (1, 2, 3)]
            x = x + (got[0] + (got[1] + got[2]))
            s += 2
        else:
            x = x + lax.ppermute(x, axis, _partner(n, s))
            s += 1
    return x + lax.ppermute(x, axis, _partner(n, 0))


def _butterfly(x, axis, n):
    for s in range(_steps(n)):
        x = x + lax.ppermute(x, axis, _partner(n, s))
    return x


def shards(solution, residual, direction, gradient, left_factors, right_factors, ranks):
    left = left_factors[:, 0, 0]
    right = right_factors[:, 0, 0]
    rounds, tile, rank_max = left.shape
    rhs = direction.shape[1]
    t_local = residual.shape[3]
    n_col = tile // t_local
    n_row = tile // direction.shape[2]
    c = lax.axis_index("col")
    r = lax.axis_index("row")
    mask = (
        jnp.arange(rank_max, dtype=jnp.int32)[None, None, :] < ranks[:, 0, 0][:, None, None]
    ).astype(jnp.float32)
    g_local = jnp.sum(gradient * gradient, axis=(0, 2))
    coeffs = (
        jnp.einsum(
            "hn,anm->ahm",
            lax.all_gather(direction, "row", axis=2, tiled=True)[0],
            right,
            precision=HIGH,
        )
        * mask
    )

    def image_part(start, size):
        rows = lax.dynamic_slice_in_dim(left, start, size, axis=1)
        part = jnp.einsum("ahm,atm->aht", coeffs, rows, precision=HIGH)
        return part.reshape(rounds * rhs, size)

    k_col = _steps(n_col)
    grid = ("row", "col")
    odd = r & 1
    if k_col >= 3:
        ar_order = ([0, 1] + list(range(2, k_col)), [1, 0] + list(range(2, k_col)))
        res_order = ([2, 0, 1] + list(range(3, k_col)), [2, 1, 0] + list(range(3, k_col)))
    else:
        ar_order = (list(range(k_col)), list(range(k_col)))
        res_order = ar_order

    def steps(order, i):
        return (order[0][i], order[1][i])

    def doubling(buf, i_steps, order):
        for i in i_steps:
            bits = steps(order, i)
            recv = lax.ppermute(buf, grid, _pair_perm(n_row, n_col, bits))
            buf = _join_lanes(_pair_bit(c, odd, bits), buf, recv)
        return buf

    extra = jnp.zeros((8, t_local), jnp.float32).at[0, :rhs].set(g_local)
    res = jnp.concatenate([residual[:, 0].reshape(rounds * rhs, t_local), extra], axis=0)
    res = doubling(res, range(k_col - 1), res_order)
    bits0 = steps(ar_order, 0)
    bit = _pair_bit(c, odd, bits0)
    half = tile // 2
    send = image_part((1 - bit) * half, half)
    res, send = lax.optimization_barrier((res, send))
    keep = image_part(bit * half, half)
    got = lax.ppermute(send, grid, _pair_perm(n_row, n_col, bits0))
    res = doubling(res, range(k_col - 1, k_col), res_order)
    res, got = lax.optimization_barrier((res, got))
    gamma_col = jnp.sum(res[rounds * rhs].reshape(n_col, t_local)[:, :rhs], axis=0)
    blocks_res = res[: rounds * rhs].reshape(rounds, rhs, n_col, t_local)
    where = [
        [sum(((d >> s) & 1) << i for i, s in enumerate(order)) for d in range(n_col)]
        for order in res_order
    ]
    where = jnp.where(odd == 0, jnp.array(where[0]), jnp.array(where[1]))
    residual_full = jnp.take(blocks_res, where, axis=2).reshape(rounds, rhs, tile)
    back_res = jnp.einsum("aht,atm->ahm", residual_full, left, precision=HIGH) * mask
    buf = keep + got
    for i in range(1, k_col):
        bits = steps(ar_order, i)
        bit = _pair_bit(c, odd, bits)
        half = buf.shape[-1] // 2
        keep = lax.dynamic_slice_in_dim(buf, bit * half, half, axis=1)
        send = lax.dynamic_slice_in_dim(buf, (1 - bit) * half, half, axis=1)
        buf = keep + lax.ppermute(send, grid, _pair_perm(n_row, n_col, bits))
    buf, back_res = lax.optimization_barrier((buf, back_res))
    p_res = jnp.einsum("ahm,anm->hn", back_res, right, precision=HIGH)
    for j, i in enumerate(reversed(range(k_col))):
        bits = steps(ar_order, i)
        if j == min(2, k_col - 1):
            buf, p_res = lax.optimization_barrier((buf, p_res))
        recv = lax.ppermute(buf, grid, _pair_perm(n_row, n_col, bits))
        buf = _join_lanes(_pair_bit(c, odd, bits), buf, recv)
    summed = buf
    image_full = summed.reshape(rounds, rhs, tile)
    d_local = jnp.sum(image_full * image_full, axis=(0, 2))
    sums = _butterfly(jnp.stack([gamma_col, d_local]), "row", n_row)
    gamma = sums[0]
    delta = sums[1]
    alpha = gamma / delta
    solution_new = solution + alpha[None, :, None] * direction
    image_mine = lax.dynamic_slice_in_dim(image_full, c * t_local, t_local, axis=2)
    residual_new = residual - alpha[None, None, :, None] * image_mine[:, None]
    back_img = jnp.einsum("aht,atm->ahm", image_full, left, precision=HIGH) * mask
    p_img = jnp.einsum("ahm,anm->hn", back_img, right, precision=HIGH)
    partial_gradient = p_res - alpha[:, None] * p_img
    k_row = _steps(n_row)
    order = [_bitrev(p, k_row) for p in range(n_row)]
    blocks = partial_gradient.reshape(rhs, n_row, tile // n_row)[:, jnp.array(order)]
    buf = blocks.reshape(rhs, tile)
    for s in range(k_row):
        bit = (r >> s) & 1
        half = buf.shape[-1] // 2
        if s < k_row - 1:
            keep = lax.dynamic_slice_in_dim(buf, bit * half, half, axis=1)
            send = lax.dynamic_slice_in_dim(buf, (1 - bit) * half, half, axis=1)
        else:
            keep, send = buf, buf
        buf = keep + lax.ppermute(send, "row", _partner(n_row, s))
    g_row = jnp.sum(buf * buf, axis=1)
    for s in range(k_row - 1):
        g_row = g_row + lax.ppermute(g_row, "row", _partner(n_row, s))
    last = (r >> (k_row - 1)) & 1
    chunk = tile // n_row
    gradient_new = lax.dynamic_slice_in_dim(buf, last * chunk, chunk, axis=1)[None]
    g_new = _radix4(g_row, "col", n_col)
    beta = g_new / gamma
    direction_new = gradient_new + beta[None, :, None] * direction
    return (solution_new, residual_new, direction_new, gradient_new)


def solution(mesh):
    return jax.shard_map(
        shards,
        mesh=mesh,
        in_specs=(
            P("col", None, "row"),
            P(None, "row", None, "col"),
            P("col", None, "row"),
            P("col", None, "row"),
            P(None, "row", "col", None, None),
            P(None, "row", "col", None, None),
            P(None, "row", "col"),
        ),
        out_specs=(
            P("col", None, "row"),
            P(None, "row", None, "col"),
            P("col", None, "row"),
            P("col", None, "row"),
        ),
        check_vma=False,
    )
```

```python
import jax
import jax.numpy as jnp
from jax import lax
from jax.sharding import PartitionSpec as P

HIGH = lax.Precision.HIGH


def _steps(n):
    k = n.bit_length() - 1
    assert (1 << k) == n
    return k


def _partner(n, s):
    return [(i, i ^ (1 << s)) for i in range(n)]


def _bitrev(i, k):
    return int(format(i, f"0{k}b")[::-1], 2) if k else 0


def _halve(buf, axis, n, idx):
    return _halve_from(buf, axis, n, idx, 0)


def _halve_from(buf, axis, n, idx, first, side=None):
    for s in range(first, _steps(n)):
        bit = (idx >> s) & 1
        half = buf.shape[-1] // 2
        keep = lax.dynamic_slice_in_dim(buf, bit * half, half, axis=buf.ndim - 1)
        send = lax.dynamic_slice_in_dim(buf, (1 - bit) * half, half, axis=buf.ndim - 1)
        if side is not None and s == first + 1:
            send, side = lax.optimization_barrier((send, side))
        buf = keep + lax.ppermute(send, axis, _partner(n, s))
    if side is not None:
        return buf, side
    return buf


def _join_lanes(bit, mine, theirs):
    return jnp.where(
        bit == 0,
        jnp.concatenate([mine, theirs], axis=-1),
        jnp.concatenate([theirs, mine], axis=-1),
    )


def _double(buf, axis, n, idx, order, side=None):
    for i, s in enumerate(order):
        bit = (idx >> s) & 1
        if side is not None and i == 1:
            buf, side = lax.optimization_barrier((buf, side))
        recv = lax.ppermute(buf, axis, _partner(n, s))
        buf = jnp.where(
            bit == 0,
            jnp.concatenate([buf, recv], axis=-1),
            jnp.concatenate([recv, buf], axis=-1),
        )
    if side is not None:
        return buf, side
    return buf


def _pair_perm(n_row, n_col, bits):
    return [
        (r * n_col + c, r * n_col + (c ^ (1 << bits[r & 1])))
        for r in range(n_row)
        for c in range(n_col)
    ]


def _pair_bit(c, odd, bits):
    return (c >> jnp.where(odd == 0, bits[0], bits[1])) & 1


def _radix4(x, axis, n):
    k = _steps(n)
    x = x + lax.ppermute(x, axis, _partner(n, 0))
    s = 1
    while s < k:
        if s + 1 < k:
            got = [lax.ppermute(x, axis, [(i, i ^ (m << s)) for i in range(n)]) for m in (1, 2, 3)]
            x = x + (got[0] + (got[1] + got[2]))
            s += 2
        else:
            x = x + lax.ppermute(x, axis, _partner(n, s))
            s += 1
    return x


def _butterfly(x, axis, n):
    for s in range(_steps(n)):
        x = x + lax.ppermute(x, axis, _partner(n, s))
    return x


def shards(solution, residual, direction, gradient, left_factors, right_factors, ranks):
    left = left_factors[:, 0, 0]
    right = right_factors[:, 0, 0]
    rounds, tile, rank_max = left.shape
    rhs = direction.shape[1]
    t_local = residual.shape[3]
    n_col = tile // t_local
    n_row = tile // direction.shape[2]
    c = lax.axis_index("col")
    r = lax.axis_index("row")
    mask = (
        jnp.arange(rank_max, dtype=jnp.int32)[None, None, :] < ranks[:, 0, 0][:, None, None]
    ).astype(jnp.float32)
    g_local = jnp.sum(gradient * gradient, axis=(0, 2))
    coeffs = (
        jnp.einsum(
            "hn,anm->ahm",
            lax.all_gather(direction, "row", axis=2, tiled=True)[0],
            right,
            precision=HIGH,
        )
        * mask
    )

    def image_part(start, size):
        rows = lax.dynamic_slice_in_dim(left, start, size, axis=1)
        part = jnp.einsum("ahm,atm->aht", coeffs, rows, precision=HIGH)
        return part.reshape(rounds * rhs, size)

    k_col = _steps(n_col)
    grid = ("row", "col")
    odd = r & 1
    if k_col >= 3:
        ar_order = ([0, 1] + list(range(2, k_col)), [1, 0] + list(range(2, k_col)))
        res_order = ([2, 0, 1] + list(range(3, k_col)), [2, 1, 0] + list(range(3, k_col)))
    else:
        ar_order = (list(range(k_col)), list(range(k_col)))
        res_order = ar_order

    def steps(order, i):
        return (order[0][i], order[1][i])

    def doubling(buf, i_steps, order):
        for i in i_steps:
            bits = steps(order, i)
            recv = lax.ppermute(buf, grid, _pair_perm(n_row, n_col, bits))
            buf = _join_lanes(_pair_bit(c, odd, bits), buf, recv)
        return buf

    extra = jnp.zeros((8, t_local), jnp.float32).at[0, :rhs].set(g_local)
    res = jnp.concatenate([residual[:, 0].reshape(rounds * rhs, t_local), extra], axis=0)
    res = doubling(res, range(k_col - 1), res_order)
    bits0 = steps(ar_order, 0)
    bit = _pair_bit(c, odd, bits0)
    half = tile // 2
    send = image_part((1 - bit) * half, half)
    res, send = lax.optimization_barrier((res, send))
    keep = image_part(bit * half, half)
    got = lax.ppermute(send, grid, _pair_perm(n_row, n_col, bits0))
    res = doubling(res, range(k_col - 1, k_col), res_order)
    res, got = lax.optimization_barrier((res, got))
    gamma_col = jnp.sum(res[rounds * rhs].reshape(n_col, t_local)[:, :rhs], axis=0)
    blocks_res = res[: rounds * rhs].reshape(rounds, rhs, n_col, t_local)
    where = [
        [sum(((d >> s) & 1) << i for i, s in enumerate(order)) for d in range(n_col)]
        for order in res_order
    ]
    where = jnp.where(odd == 0, jnp.array(where[0]), jnp.array(where[1]))
    residual_full = jnp.take(blocks_res, where, axis=2).reshape(rounds, rhs, tile)
    back_res = jnp.einsum("aht,atm->ahm", residual_full, left, precision=HIGH) * mask
    buf = keep + got
    for i in range(1, k_col):
        bits = steps(ar_order, i)
        bit = _pair_bit(c, odd, bits)
        half = buf.shape[-1] // 2
        keep = lax.dynamic_slice_in_dim(buf, bit * half, half, axis=1)
        send = lax.dynamic_slice_in_dim(buf, (1 - bit) * half, half, axis=1)
        buf = keep + lax.ppermute(send, grid, _pair_perm(n_row, n_col, bits))
    buf, back_res = lax.optimization_barrier((buf, back_res))
    p_res = jnp.einsum("ahm,anm->hn", back_res, right, precision=HIGH)
    for j, i in enumerate(reversed(range(k_col))):
        bits = steps(ar_order, i)
        recv = lax.ppermute(buf, grid, _pair_perm(n_row, n_col, bits))
        buf = _join_lanes(_pair_bit(c, odd, bits), buf, recv)
    summed = buf
    image_full = summed.reshape(rounds, rhs, tile)
    d_local = jnp.sum(image_full * image_full, axis=(0, 2))
    sums = _butterfly(jnp.stack([gamma_col, d_local]), "row", n_row)
    gamma = sums[0]
    delta = sums[1]
    alpha = gamma / delta
    solution_new = solution + alpha[None, :, None] * direction
    image_mine = lax.dynamic_slice_in_dim(image_full, c * t_local, t_local, axis=2)
    residual_new = residual - alpha[None, None, :, None] * image_mine[:, None]
    back_img = jnp.einsum("aht,atm->ahm", image_full, left, precision=HIGH) * mask
    p_img = jnp.einsum("ahm,anm->hn", back_img, right, precision=HIGH)
    partial_gradient = p_res - alpha[:, None] * p_img
    k_row = _steps(n_row)
    order = [_bitrev(p, k_row) for p in range(n_row)]
    blocks = partial_gradient.reshape(rhs, n_row, tile // n_row)[:, jnp.array(order)]
    buf = blocks.reshape(rhs, tile)
    for s in range(k_row):
        bit = (r >> s) & 1
        half = buf.shape[-1] // 2
        if s < k_row - 1:
            keep = lax.dynamic_slice_in_dim(buf, bit * half, half, axis=1)
            send = lax.dynamic_slice_in_dim(buf, (1 - bit) * half, half, axis=1)
        else:
            keep, send = buf, buf
        buf = keep + lax.ppermute(send, "row", _partner(n_row, s))
    g_row = jnp.sum(buf * buf, axis=1)
    for s in range(k_row - 1):
        g_row = g_row + lax.ppermute(g_row, "row", _partner(n_row, s))
    last = (r >> (k_row - 1)) & 1
    chunk = tile // n_row
    gradient_new = lax.dynamic_slice_in_dim(buf, last * chunk, chunk, axis=1)[None]
    g_new = _radix4(g_row, "col", n_col)
    beta = g_new / gamma
    direction_new = gradient_new + beta[None, :, None] * direction
    return (solution_new, residual_new, direction_new, gradient_new)


def solution(mesh):
    return jax.shard_map(
        shards,
        mesh=mesh,
        in_specs=(
            P("col", None, "row"),
            P(None, "row", None, "col"),
            P("col", None, "row"),
            P("col", None, "row"),
            P(None, "row", "col", None, None),
            P(None, "row", "col", None, None),
            P(None, "row", "col"),
        ),
        out_specs=(
            P("col", None, "row"),
            P(None, "row", None, "col"),
            P("col", None, "row"),
            P("col", None, "row"),
        ),
        check_vma=False,
    )
```
